32 devices in a mesh: dom: 8 (over z, y), rep: 4 (over x, core).
Axes of the slice: x: 2, y: 2, z: 4, core: 2. Of those that a mesh axis runs over, the one named last changes fastest.
Arguments:
- features_t: float32 [256, 16384], P('rep', 'dom'), may hold values from -6 to 6
- tiles: bfloat16 [8, 8, 128, 128], P('dom', 'rep'), may hold values from -0.5 to 0.5
- send_block: int32 [8, 8], P('dom'), may hold values from 0 to 15
- tile_row: int32 [8, 8], P('dom'), may hold values from 0 to 15
- order: int32 [8, 2048], P('dom'), may hold values from 0 to 2047, each once within a row
- labels: int32 [16384], P(('dom', 'rep')), may hold values 0 or 1
- w_first: bfloat16 [512, 1024], replicated, may hold values from -0.25 to 0.25
- w_score: float32 [1024], replicated, may hold values from -0.1875 to 0.1875
Outputs:
- hop_out: float32 [256, 16384], P('rep', 'dom')
- scores: float32 [16384], P(('dom', 'rep'))
- grad_first: float32 [512, 1024], P('rep')
The draws below stay inside these ranges and needn't reach their ends.
Inputs may be any that keep to these rules, and one draw needn't show every extreme that they name: Each row of order is a permutation of the nodes of one index of dom.
All inputs are finite; a program needn't handle non-finite values. No bound on the sum of `labels` on one device may be relied on, other than what follows from the above.
Results may differ from the reference program's by a relative error of at most 0.003.
Values may be sent and summed in bfloat16 or wider, within the bound.
No kernel may reach another device: no remote copies, remote signals or barrier semaphores. Data moves between devices by JAX's collectives and lax.ppermute only.
A program may use at most 64 MiB of HBM per device.

```python
import jax
import jax.numpy as jnp
from jax import lax

F = 256
FF = 1024
TILE = 128
ROWS_DEV = 2048
RB = 16
NODES = 16384
SAMPLES_DEV = 512
PER = 256
N_DOM = 8
N_REP = 4


def plant(array, key, least, largest):
    shape = array.shape
    index_at = [jax.random.randint(jax.random.fold_in(key, axis), (), 0, shape[axis]) for axis in range(len(shape))]
    array = array.at[tuple(index_at)].set(least)
    longest = shape.index(max(shape))
    index_at[longest] = (index_at[longest] + 1) % shape[longest]
    return array.at[tuple(index_at)].set(largest)


def steps_of(stream_key, dims, shards, smallest, largest):
    loudness = 1.0
    for position, parts in shards:
        heights = jax.random.uniform(jax.random.fold_in(jax.random.fold_in(stream_key, 6), position), (parts,), jnp.float32, smallest / len(shards), largest / len(shards))
        loudness = loudness * jnp.repeat(jnp.exp(heights), dims[position] // parts).reshape((-1,) + (1,) * (len(dims) - 1 - position))
    return loudness


def noise(own_key, dims, scale, limit, pieces=(), kind=jnp.bfloat16):
    factor_of = steps_of(own_key, dims, pieces, -0.22, 0.18) if pieces else 1.0
    array = jax.random.normal(own_key, dims, jnp.float32) * scale * factor_of
    return jnp.minimum(jnp.maximum(array, -limit), limit).astype(kind)


def setup_inputs(seed: int = 0) -> dict:
    keys = jax.random.split(jax.random.key(seed), 9)
    features_t = noise(keys[0], (F, NODES), 1.0, 6.0, ((0, 4), (1, 8)), jnp.float32)
    tiles = noise(keys[1], (N_DOM, N_DOM, TILE, TILE), (max(TILE, TILE * N_DOM // RB)) ** -0.5, 0.5, ((0, 8), (1, 4)))
    send_block = plant(jax.random.randint(keys[2], (N_DOM, N_DOM), 0, RB), jax.random.fold_in(keys[2], 1), 0, RB - 1).astype(jnp.int32)
    tile_row = plant(jax.random.randint(keys[3], (N_DOM, N_DOM), 0, RB), jax.random.fold_in(keys[3], 1), 0, RB - 1).astype(jnp.int32)
    order = jax.vmap(lambda own: jax.random.permutation(own, ROWS_DEV))(jax.random.split(keys[4], N_DOM)).reshape((N_DOM, ROWS_DEV)).astype(jnp.int32)
    labels = plant((jax.random.randint(keys[5], (NODES,), 0, 4) < 1).astype(jnp.int32), jax.random.fold_in(keys[5], 1), 0, 1)
    w_first = noise(keys[6], (2 * F, FF), (2 * F) ** -0.5, 0.25)
    w_score = noise(keys[7], (FF,), FF ** -0.5, 0.1875, (), jnp.float32)
    return dict(features_t=features_t, tiles=tiles, send_block=send_block, tile_row=tile_row, order=order, labels=labels, w_first=w_first, w_score=w_score)


def reference(features_t, tiles, send_block, tile_row, order, labels, w_first, w_score):
    feat_blocks = features_t.reshape(F, N_DOM, RB, TILE)
    sources = jnp.arange(N_DOM, dtype=jnp.int32)
    block_ids = jnp.arange(RB, dtype=jnp.int32)

    def per_dst(dst):
        picked = feat_blocks[:, sources, send_block[:, dst], :]
        product_terms = jnp.einsum("fjc,jrc->jfr", picked, tiles[dst].astype(jnp.float32), precision=lax.Precision.HIGHEST)
        spread = (tile_row[dst][:, None] == block_ids[None, :]).astype(jnp.float32)
        return jnp.einsum("jb,jfr->fbr", spread, product_terms, precision=lax.Precision.HIGHEST)

    hopped = lax.map(per_dst, sources)
    hop_out = jnp.transpose(hopped, (1, 0, 2, 3)).reshape(F, NODES)

    offsets = (sources * ROWS_DEV)[:, None, None]
    node_index = order.reshape(N_DOM, N_DOM, PER).astype(jnp.int32) + offsets
    node_index = jnp.transpose(node_index, (1, 0, 2)).reshape(N_DOM * N_REP, SAMPLES_DEV)
    plain_rows = features_t.astype(jnp.bfloat16)
    hop_rows = hop_out.astype(jnp.bfloat16)
    weight_first = w_first.astype(jnp.float32)

    def scan_step(accum, pair):
        sample_index, label_part = pair
        inputs = jnp.concatenate([jnp.take(plain_rows, sample_index, axis=1), jnp.take(hop_rows, sample_index, axis=1)], axis=0)
        inputs = inputs.astype(jnp.float32)
        pre = jnp.dot(inputs.T, weight_first, precision=lax.Precision.HIGHEST)
        gate = jax.nn.sigmoid(pre)
        scores = jnp.dot(pre * gate, w_score, precision=lax.Precision.HIGHEST)
        error_term = jax.nn.sigmoid(scores) - label_part.astype(jnp.float32)
        derivative = gate * (1.0 + pre * (1.0 - gate))
        back = (error_term[:, None] * w_score[None, :] * derivative).astype(jnp.bfloat16)
        back = lax.optimization_barrier(back).astype(jnp.float32)
        return accum + jnp.dot(inputs, back, precision=lax.Precision.HIGHEST), scores

    grad_first, scores = lax.scan(scan_step, jnp.zeros((2 * F, FF), jnp.float32), (node_index, labels.reshape(N_DOM * N_REP, SAMPLES_DEV)))
    return hop_out, scores.reshape(NODES), grad_first
```

```python
import jax
import jax.numpy as jnp
from jax import lax
from jax.sharding import PartitionSpec as P


def hop_terms(source_rows, tile_piece, spread):
    product_terms = jnp.einsum(
        "fjc,jrc->jfr", source_rows, tile_piece.astype(jnp.float32), precision=lax.Precision.HIGHEST
    )
    return jnp.einsum("jb,jfr->fbr", spread, product_terms, precision=lax.Precision.HIGHEST)


def reduce_rows(local_grad, dom_size, rep_size):
    rows, cols = local_grad.shape
    piece = rows // (rep_size * dom_size)
    parts = local_grad.reshape(rep_size, dom_size, piece, cols)
    parts = lax.all_to_all(parts, "rep", 0, 0, tiled=True).sum(0)
    parts = lax.all_to_all(parts, "dom", 0, 0, tiled=True).sum(0)
    copies = jnp.broadcast_to(parts[None], (dom_size, piece, cols))
    return lax.all_to_all(copies, "dom", 0, 0, tiled=True).reshape(dom_size * piece, cols)


def on_device(features_t, tiles, send_block, tile_row, order, labels, w_first, w_score):
    feat_cols, row_count = features_t.shape
    tile_size = tiles.shape[-1]
    block_count = row_count // tile_size
    dom_size = lax.axis_size("dom")
    rep_size = lax.axis_size("rep")
    node_blocks = features_t.reshape(feat_cols, block_count, tile_size)
    outgoing = jnp.take(node_blocks, send_block[0], axis=1)
    block_ids = jnp.arange(block_count, dtype=jnp.int32)
    placed = (tile_row[0][:, None] == block_ids[None, :]).astype(jnp.float32)
    local_tiles = tiles[0]
    arrived = lax.all_to_all(outgoing, "dom", split_axis=1, concat_axis=1, tiled=True)
    hopped = hop_terms(arrived, lax.all_gather(local_tiles, "rep", axis=0, tiled=True), placed)
    hop_out = hopped.reshape(feat_cols, row_count)
    sample_index = order[0]
    per_owner = row_count // dom_size

    def arrange(values):
        return jnp.take(values, sample_index, axis=1).reshape(feat_cols, dom_size, per_owner)

    plain_rows = arrange(features_t.astype(jnp.bfloat16))
    hop_rows = arrange(hop_out.astype(jnp.bfloat16))
    plain_got, hop_got = (
        lax.all_to_all(
            lax.all_to_all(plain_rows, "dom", split_axis=1, concat_axis=1, tiled=True),
            "rep",
            split_axis=1,
            concat_axis=0,
            tiled=True,
        ),
        lax.all_to_all(
            lax.all_to_all(hop_rows, "dom", split_axis=1, concat_axis=1, tiled=True),
            "rep",
            split_axis=1,
            concat_axis=0,
            tiled=True,
        ),
    )
    sample_total = plain_got.shape[1] * plain_got.shape[2]
    inputs = jnp.concatenate(
        [plain_got.reshape(-1, sample_total), hop_got.reshape(-1, sample_total)], axis=0
    )
    pre = lax.dot_general(
        inputs, w_first, (((0,), (0,)), ((), ())), preferred_element_type=jnp.float32
    )
    gate = jax.nn.sigmoid(pre)
    scores = jnp.dot(pre * gate, w_score, precision=lax.Precision.HIGHEST)
    error_term = jax.nn.sigmoid(scores) - labels.astype(jnp.float32)
    derivative = gate * (1.0 + pre * (1.0 - gate))
    back = (error_term[:, None] * w_score[None, :] * derivative).astype(jnp.bfloat16)
    local_grad = jnp.dot(inputs, back, preferred_element_type=jnp.float32)
    gradient = reduce_rows(local_grad, dom_size, rep_size)
    return (hop_out, scores, gradient)


def solution(mesh):
    placed = (
        P("rep", "dom"),
        P("dom", "rep", None, None),
        P("dom", None),
        P("dom", None),
        P("dom", None),
        P(("dom", "rep")),
        P(),
        P(),
    )
    return jax.shard_map(
        on_device,
        mesh=mesh,
        in_specs=placed,
        out_specs=(P("rep", "dom"), P(("dom", "rep")), P("rep", None)),
        check_vma=False,
    )
```

```python
import jax
import jax.numpy as jnp
from jax import lax
from jax.sharding import PartitionSpec as P


def hop_terms(source_rows, tile_piece, spread):
    product_terms = jnp.einsum(
        "fjc,jrc->jfr", source_rows, tile_piece.astype(jnp.float32), precision=lax.Precision.HIGHEST
    )
    return jnp.einsum("jb,jfr->fbr", spread, product_terms, precision=lax.Precision.HIGHEST)


def gather_all(values, axes, count):
    copies = jnp.broadcast_to(values[None], (count,) + values.shape)
    return lax.all_to_all(copies, axes, 0, 0, tiled=True).reshape((count * values.shape[0],) + values.shape[1:])


def halve(values, axis, size):
    index = lax.axis_index(axis)
    values = values.reshape((size, values.shape[0] // size) + values.shape[1:])
    step = 0
    while (1 << step) < size:
        bit = (index >> step) & 1
        pairs = values.reshape((values.shape[0] // 2, 2) + values.shape[1:])
        keep = lax.dynamic_index_in_dim(pairs, bit, 1, keepdims=False)
        give = lax.dynamic_index_in_dim(pairs, 1 - bit, 1, keepdims=False)
        values = keep + lax.ppermute(give, axis, [(i, i ^ (1 << step)) for i in range(size)])
        step += 1
    return values[0]


def reduce_rows(local_grad, dom_size, rep_size):
    rows, cols = local_grad.shape
    piece = rows // (rep_size * dom_size)
    if rep_size & (rep_size - 1) == 0 and dom_size & (dom_size - 1) == 0:
        parts = halve(halve(local_grad, "rep", rep_size), "dom", dom_size)
    else:
        parts = local_grad.reshape(rep_size, dom_size, piece, cols)
        parts = lax.all_to_all(parts, "rep", 0, 0, tiled=True).sum(0)
        parts = lax.all_to_all(parts, "dom", 0, 0, tiled=True).sum(0)
    return gather_all(parts, "dom", dom_size)


def on_device(features_t, tiles, send_block, tile_row, order, labels, w_first, w_score):
    feat_cols, row_count = features_t.shape
    tile_size = tiles.shape[-1]
    block_count = row_count // tile_size
    dom_size = lax.axis_size("dom")
    rep_size = lax.axis_size("rep")
    dom_at = lax.axis_index("dom")
    rep_at = lax.axis_index("rep")
    node_blocks = features_t.reshape(feat_cols, block_count, tile_size)
    outgoing = jnp.take(node_blocks, send_block[0], axis=1)
    block_ids = jnp.arange(block_count, dtype=jnp.int32)
    placed = (tile_row[0][:, None] == block_ids[None, :]).astype(jnp.float32)
    local_tiles = tiles[0]
    arrived = lax.all_to_all(outgoing, "dom", split_axis=1, concat_axis=1, tiled=True)
    hopped = hop_terms(arrived, lax.all_gather(local_tiles, "rep", axis=0, tiled=True), placed)
    hop_out = hopped.reshape(feat_cols, row_count)

    per_dev = labels.shape[0]
    per_owner = row_count // dom_size
    owners_here = per_dev // per_owner
    rows_here = jnp.concatenate([features_t.astype(jnp.bfloat16), hop_out.astype(jnp.bfloat16)], axis=0)
    picked = jnp.take(rows_here, order[0], axis=1)
    got = lax.all_to_all(picked, "rep", split_axis=1, concat_axis=0, tiled=True)
    inputs = got.reshape(rep_size, 2, feat_cols, per_dev).transpose(1, 0, 2, 3).reshape(-1, per_dev)

    device_count = dom_size * rep_size
    all_labels = gather_all(labels.astype(jnp.float32), ("dom", "rep"), device_count)
    all_labels = all_labels.reshape(dom_size, dom_size, per_owner)
    label_part = lax.dynamic_slice(
        all_labels, (rep_at * owners_here, dom_at, 0), (owners_here, 1, per_owner)
    ).reshape(per_dev)

    pre = lax.dot_general(
        inputs, w_first, (((0,), (0,)), ((), ())), preferred_element_type=jnp.float32
    )
    gate = jax.nn.sigmoid(pre)
    scores = jnp.dot(pre * gate, w_score, precision=lax.Precision.HIGHEST)
    error_term = jax.nn.sigmoid(scores) - label_part
    derivative = gate * (1.0 + pre * (1.0 - gate))
    back = (error_term[:, None] * w_score[None, :] * derivative).astype(jnp.bfloat16)
    local_grad = jnp.dot(inputs, back, preferred_element_type=jnp.float32)
    gradient = reduce_rows(local_grad, dom_size, rep_size)

    all_scores = gather_all(scores, ("dom", "rep"), device_count)
    all_scores = all_scores.reshape(dom_size, rep_size, owners_here, per_owner)
    own_scores = lax.dynamic_slice(
        all_scores,
        (rep_at * owners_here, dom_at // owners_here, dom_at % owners_here, 0),
        (owners_here, 1, 1, per_owner),
    ).reshape(per_dev)
    return (hop_out, own_scores, gradient)


def solution(mesh):
    placed = (
        P("rep", "dom"),
        P("dom", "rep", None, None),
        P("dom", None),
        P("dom", None),
        P("dom", None),
        P(("dom", "rep")),
        P(),
        P(),
    )
    return jax.shard_map(
        on_device,
        mesh=mesh,
        in_specs=placed,
        out_specs=(P("rep", "dom"), P(("dom", "rep")), P("rep", None)),
        check_vma=False,
    )
```

```python
import jax
import jax.numpy as jnp
from jax import lax
from jax.sharding import PartitionSpec as P


def hop_terms(source_rows, tile_piece, spread):
    product_terms = jnp.einsum(
        "fjc,jrc->jfr", source_rows, tile_piece.astype(jnp.float32), precision=lax.Precision.HIGHEST
    )
    return jnp.einsum("jb,jfr->fbr", spread, product_terms, precision=lax.Precision.HIGHEST)


def gather_all(values, axes, count):
    copies = jnp.broadcast_to(values[None], (count,) + values.shape)
    return lax.all_to_all(copies, axes, 0, 0, tiled=True).reshape((count * values.shape[0],) + values.shape[1:])


def halve(values, axis, size):
    index = lax.axis_index(axis)
    values = values.reshape((size, values.shape[0] // size) + values.shape[1:])
    step = 0
    while (1 << step) < size:
        bit = (index >> step) & 1
        pairs = values.reshape((values.shape[0] // 2, 2) + values.shape[1:])
        keep = lax.dynamic_index_in_dim(pairs, bit, 1, keepdims=False)
        give = lax.dynamic_index_in_dim(pairs, 1 - bit, 1, keepdims=False)
        values = keep + lax.ppermute(give, axis, [(i, i ^ (1 << step)) for i in range(size)])
        step += 1
    return values[0]


def reduce_rows(local_grad, dom_size, rep_size):
    rows, cols = local_grad.shape
    piece = rows // (rep_size * dom_size)
    if rep_size & (rep_size - 1) == 0 and dom_size & (dom_size - 1) == 0:
        parts = halve(halve(local_grad, "rep", rep_size), "dom", dom_size)
    else:
        parts = local_grad.reshape(rep_size, dom_size, piece, cols)
        parts = lax.all_to_all(parts, "rep", 0, 0, tiled=True).sum(0)
        parts = lax.all_to_all(parts, "dom", 0, 0, tiled=True).sum(0)
    return gather_all(parts, "dom", dom_size)


def on_device(features_t, tiles, send_block, tile_row, order, labels, w_first, w_score):
    feat_cols, row_count = features_t.shape
    tile_size = tiles.shape[-1]
    block_count = row_count // tile_size
    dom_size = lax.axis_size("dom")
    rep_size = lax.axis_size("rep")
    dom_at = lax.axis_index("dom")
    rep_at = lax.axis_index("rep")
    node_blocks = features_t.reshape(feat_cols, block_count, tile_size)
    outgoing = jnp.take(node_blocks, send_block[0], axis=1)
    block_ids = jnp.arange(block_count, dtype=jnp.int32)
    placed = (tile_row[0][:, None] == block_ids[None, :]).astype(jnp.float32)
    local_tiles = tiles[0]
    arrived = lax.all_to_all(outgoing, "dom", split_axis=1, concat_axis=1, tiled=True)
    hopped = hop_terms(arrived, lax.all_gather(local_tiles, "rep", axis=0, tiled=True), placed)
    hop_out = hopped.reshape(feat_cols, row_count)

    per_dev = labels.shape[0]
    per_owner = row_count // dom_size
    owners_here = per_dev // per_owner
    chunk_ids = jnp.arange(owners_here, dtype=jnp.int32)
    rotated = (chunk_ids + dom_at) % owners_here
    node_ids = order[0].reshape(rep_size, owners_here, per_owner)
    node_ids = jnp.take(node_ids, rotated, axis=1).reshape(row_count)
    rows_here = jnp.concatenate([features_t.astype(jnp.bfloat16), hop_out.astype(jnp.bfloat16)], axis=0)
    picked = jnp.take(rows_here, node_ids, axis=1)
    got = lax.all_to_all(picked, "rep", split_axis=1, concat_axis=0, tiled=True)
    inputs = got.reshape(rep_size, 2, feat_cols, per_dev).transpose(1, 0, 2, 3).reshape(-1, per_dev)

    def score_pairs(k):
        pairs = []
        for j in range(dom_size):
            for r in range(rep_size):
                owner = (r * owners_here + (k + j) % owners_here) * rep_size + j // owners_here
                pairs.append((j * rep_size + r, owner))
        return pairs

    label_rows = labels.astype(jnp.float32).reshape(owners_here, per_owner)
    sent_at = (dom_at % owners_here - chunk_ids) % owners_here
    label_part = jnp.concatenate(
        [
            lax.ppermute(label_rows[sent_at[k]], ("dom", "rep"), [(b, a) for a, b in score_pairs(k)])
            for k in range(owners_here)
        ]
    )

    pre = lax.dot_general(
        inputs, w_first, (((0,), (0,)), ((), ())), preferred_element_type=jnp.float32
    )
    gate = jax.nn.sigmoid(pre)
    scores = jnp.dot(pre * gate, w_score, precision=lax.Precision.HIGHEST)
    error_term = jax.nn.sigmoid(scores) - label_part
    derivative = gate * (1.0 + pre * (1.0 - gate))
    back = (error_term[:, None] * w_score[None, :] * derivative).astype(jnp.bfloat16)
    local_grad = jnp.dot(inputs, back, preferred_element_type=jnp.float32)
    gradient = reduce_rows(local_grad, dom_size, rep_size)

    score_rows = scores.reshape(owners_here, per_owner)
    returned = jnp.stack(
        [lax.ppermute(score_rows[k], ("dom", "rep"), score_pairs(k)) for k in range(owners_here)]
    )
    own_scores = jnp.take(returned, sent_at, axis=0).reshape(per_dev)
    return (hop_out, own_scores, gradient)


def solution(mesh):
    placed = (
        P("rep", "dom"),
        P("dom", "rep", None, None),
        P("dom", None),
        P("dom", None),
        P("dom", None),
        P(("dom", "rep")),
        P(),
        P(),
    )
    return jax.shard_map(
        on_device,
        mesh=mesh,
        in_specs=placed,
        out_specs=(P("rep", "dom"), P(("dom", "rep")), P("rep", None)),
        check_vma=False,
    )
```

```python
import jax
import jax.numpy as jnp
from jax import lax
from jax.sharding import PartitionSpec as P


def hop_terms(source_rows, tile_piece, spread):
    product_terms = jnp.einsum(
        "fjc,jrc->jfr", source_rows, tile_piece.astype(jnp.float32), precision=lax.Precision.HIGHEST
    )
    return jnp.einsum("jb,jfr->fbr", spread, product_terms, precision=lax.Precision.HIGHEST)


def gather_all(values, axes, count):
    copies = jnp.broadcast_to(values[None], (count,) + values.shape)
    return lax.all_to_all(copies, axes, 0, 0, tiled=True).reshape((count * values.shape[0],) + values.shape[1:])


def halve_in_order(values, steps, bit_names, sizes):
    names = list(bit_names)
    values = values.reshape((2,) * len(names) + (values.shape[0] >> len(names),) + values.shape[1:])
    for name in steps:
        axis, bit_at = name
        position = names.index(name)
        bit = (lax.axis_index(axis) >> bit_at) & 1
        keep = lax.dynamic_index_in_dim(values, bit, position, keepdims=False)
        give = lax.dynamic_index_in_dim(values, 1 - bit, position, keepdims=False)
        pairs = [(i, i ^ (1 << bit_at)) for i in range(sizes[axis])]
        values = keep + lax.ppermute(give, axis, pairs)
        names.pop(position)
    return values


def reduce_rows(local_grad, dom_size, rep_size):
    rows, cols = local_grad.shape
    piece = rows // (rep_size * dom_size)
    if rep_size & (rep_size - 1) == 0 and dom_size & (dom_size - 1) == 0 and cols % 2 == 0:
        rep_bits = [("rep", b) for b in range(rep_size.bit_length() - 1)]
        dom_bits = [("dom", b) for b in range(dom_size.bit_length() - 1)]
        bit_names = rep_bits[::-1] + dom_bits[::-1]
        sizes = {"rep": rep_size, "dom": dom_size}
        first = halve_in_order(local_grad[:, : cols // 2], rep_bits + dom_bits, bit_names, sizes)
        second = halve_in_order(local_grad[:, cols // 2 :], rep_bits[:1] + dom_bits + rep_bits[1:], bit_names, sizes)
        parts = jnp.concatenate([first, second], axis=-1)
    else:
        parts = local_grad.reshape(rep_size, dom_size, piece, cols)
        parts = lax.all_to_all(parts, "rep", 0, 0, tiled=True).sum(0)
        parts = lax.all_to_all(parts, "dom", 0, 0, tiled=True).sum(0)
    return gather_all(parts, "dom", dom_size)


def on_device(features_t, tiles, send_block, tile_row, order, labels, w_first, w_score):
    feat_cols, row_count = features_t.shape
    tile_size = tiles.shape[-1]
    block_count = row_count // tile_size
    dom_size = lax.axis_size("dom")
    rep_size = lax.axis_size("rep")
    dom_at = lax.axis_index("dom")
    rep_at = lax.axis_index("rep")
    node_blocks = features_t.reshape(feat_cols, block_count, tile_size)
    outgoing = jnp.take(node_blocks, send_block[0], axis=1)
    block_ids = jnp.arange(block_count, dtype=jnp.int32)
    placed = (tile_row[0][:, None] == block_ids[None, :]).astype(jnp.float32)
    local_tiles = tiles[0]
    arrived = lax.all_to_all(outgoing, "dom", split_axis=1, concat_axis=1, tiled=True)
    hopped = hop_terms(arrived, lax.all_gather(local_tiles, "rep", axis=0, tiled=True), placed)
    hop_out = hopped.reshape(feat_cols, row_count)

    per_dev = labels.shape[0]
    per_owner = row_count // dom_size
    owners_here = per_dev // per_owner
    chunk_ids = jnp.arange(owners_here, dtype=jnp.int32)
    rotated = (chunk_ids + dom_at) % owners_here
    node_ids = order[0].reshape(rep_size, owners_here, per_owner)
    node_ids = jnp.take(node_ids, rotated, axis=1).reshape(row_count)
    rows_here = jnp.concatenate([features_t.astype(jnp.bfloat16), hop_out.astype(jnp.bfloat16)], axis=0)
    picked = jnp.take(rows_here, node_ids, axis=1)
    got = lax.all_to_all(picked, "rep", split_axis=1, concat_axis=0, tiled=True)
    inputs = got.reshape(rep_size, 2, feat_cols, per_dev).transpose(1, 0, 2, 3).reshape(-1, per_dev)

    def score_pairs(k):
        pairs = []
        for j in range(dom_size):
            for r in range(rep_size):
                owner = (r * owners_here + (k + j) % owners_here) * rep_size + j // owners_here
                pairs.append((j * rep_size + r, owner))
        return pairs

    label_rows = labels.astype(jnp.float32).reshape(owners_here, per_owner)
    sent_at = (dom_at % owners_here - chunk_ids) % owners_here
    label_part = jnp.concatenate(
        [
            lax.ppermute(label_rows[sent_at[k]], ("dom", "rep"), [(b, a) for a, b in score_pairs(k)])
            for k in range(owners_here)
        ]
    )

    pre = lax.dot_general(
        inputs, w_first, (((0,), (0,)), ((), ())), preferred_element_type=jnp.float32
    )
    gate = jax.nn.sigmoid(pre)
    scores = jnp.dot(pre * gate, w_score, precision=lax.Precision.HIGHEST)
    error_term = jax.nn.sigmoid(scores) - label_part
    derivative = gate * (1.0 + pre * (1.0 - gate))
    back = (error_term[:, None] * w_score[None, :] * derivative).astype(jnp.bfloat16)
    local_grad = jnp.dot(inputs, back, preferred_element_type=jnp.float32)
    gradient = reduce_rows(local_grad, dom_size, rep_size)

    score_rows = scores.reshape(owners_here, per_owner)
    returned = jnp.stack(
        [lax.ppermute(score_rows[k], ("dom", "rep"), score_pairs(k)) for k in range(owners_here)]
    )
    own_scores = jnp.take(returned, sent_at, axis=0).reshape(per_dev)
    return (hop_out, own_scores, gradient)


def solution(mesh):
    placed = (
        P("rep", "dom"),
        P("dom", "rep", None, None),
        P("dom", None),
        P("dom", None),
        P("dom", None),
        P(("dom", "rep")),
        P(),
        P(),
    )
    return jax.shard_map(
        on_device,
        mesh=mesh,
        in_specs=placed,
        out_specs=(P("rep", "dom"), P(("dom", "rep")), P("rep", None)),
        check_vma=False,
    )
```

```python
import jax
import jax.numpy as jnp
from jax import lax
from jax.sharding import PartitionSpec as P


def hop_terms(source_rows, tile_piece, spread):
    product_terms = jnp.einsum(
        "fjc,jrc->jfr", source_rows, tile_piece.astype(jnp.float32), precision=lax.Precision.HIGHEST
    )
    return jnp.einsum("jb,jfr->fbr", spread, product_terms, precision=lax.Precision.HIGHEST)


def gather_all(values, axes, count):
    copies = jnp.broadcast_to(values[None], (count,) + values.shape)
    return lax.all_to_all(copies, axes, 0, 0, tiled=True).reshape((count * values.shape[0],) + values.shape[1:])


def halve_in_order(values, steps, bit_names, sizes):
    names = list(bit_names)
    values = values.reshape((2,) * len(names) + (values.shape[0] >> len(names),) + values.shape[1:])
    for name in steps:
        axis, bit_at = name
        position = names.index(name)
        bit = (lax.axis_index(axis) >> bit_at) & 1
        keep = lax.dynamic_index_in_dim(values, bit, position, keepdims=False)
        give = lax.dynamic_index_in_dim(values, 1 - bit, position, keepdims=False)
        pairs = [(i, i ^ (1 << bit_at)) for i in range(sizes[axis])]
        values = keep + lax.ppermute(give, axis, pairs)
        names.pop(position)
    return values


def reduce_rows(local_grad, dom_size, rep_size):
    rows, cols = local_grad.shape
    piece = rows // (rep_size * dom_size)
    if rep_size & (rep_size - 1) == 0 and dom_size & (dom_size - 1) == 0 and cols % 2 == 0:
        rep_bits = [("rep", b) for b in range(rep_size.bit_length() - 1)]
        dom_bits = [("dom", b) for b in range(dom_size.bit_length() - 1)]
        bit_names = rep_bits[::-1] + dom_bits[::-1]
        sizes = {"rep": rep_size, "dom": dom_size}
        first = halve_in_order(local_grad[:, : cols // 2], rep_bits + dom_bits, bit_names, sizes)
        second = halve_in_order(local_grad[:, cols // 2 :], rep_bits[:1] + dom_bits + rep_bits[1:], bit_names, sizes)
        parts = jnp.concatenate([first, second], axis=-1)
    else:
        parts = local_grad.reshape(rep_size, dom_size, piece, cols)
        parts = lax.all_to_all(parts, "rep", 0, 0, tiled=True).sum(0)
        parts = lax.all_to_all(parts, "dom", 0, 0, tiled=True).sum(0)
    return gather_all(parts, "dom", dom_size)


def on_device(features_t, tiles, send_block, tile_row, order, labels, w_first, w_score):
    feat_cols, row_count = features_t.shape
    tile_size = tiles.shape[-1]
    block_count = row_count // tile_size
    dom_size = lax.axis_size("dom")
    rep_size = lax.axis_size("rep")
    dom_at = lax.axis_index("dom")
    rep_at = lax.axis_index("rep")
    node_blocks = features_t.reshape(feat_cols, block_count, tile_size)
    outgoing = jnp.take(node_blocks, send_block[0], axis=1)
    block_ids = jnp.arange(block_count, dtype=jnp.int32)
    placed = (tile_row[0][:, None] == block_ids[None, :]).astype(jnp.float32)
    local_tiles = tiles[0]
    arrived = lax.all_to_all(outgoing, "dom", split_axis=1, concat_axis=1, tiled=True)
    hopped = hop_terms(arrived, lax.all_gather(local_tiles, "rep", axis=0, tiled=True), placed)
    hop_out = hopped.reshape(feat_cols, row_count)

    per_dev = labels.shape[0]
    per_owner = row_count // dom_size
    owners_here = per_dev // per_owner
    chunk_ids = jnp.arange(owners_here, dtype=jnp.int32)
    rotated = (chunk_ids + dom_at) % owners_here
    node_ids = order[0].reshape(rep_size, owners_here, per_owner)
    node_ids = jnp.take(node_ids, rotated, axis=1).reshape(row_count)
    rows_here = jnp.concatenate([features_t.astype(jnp.bfloat16), hop_out.astype(jnp.bfloat16)], axis=0)
    select = (jnp.arange(row_count, dtype=jnp.int32)[:, None] == node_ids[None, :]).astype(jnp.bfloat16)
    picked = jnp.dot(rows_here, select, preferred_element_type=jnp.float32).astype(jnp.bfloat16)
    got = lax.all_to_all(picked, "rep", split_axis=1, concat_axis=0, tiled=True)
    inputs = got.reshape(rep_size, 2, feat_cols, per_dev).transpose(1, 0, 2, 3).reshape(-1, per_dev)

    def score_pairs(k):
        pairs = []
        for j in range(dom_size):
            for r in range(rep_size):
                owner = (r * owners_here + (k + j) % owners_here) * rep_size + j // owners_here
                pairs.append((j * rep_size + r, owner))
        return pairs

    label_rows = labels.astype(jnp.float32).reshape(owners_here, per_owner)
    sent_at = (dom_at % owners_here - chunk_ids) % owners_here
    label_part = jnp.concatenate(
        [
            lax.ppermute(label_rows[sent_at[k]], ("dom", "rep"), [(b, a) for a, b in score_pairs(k)])
            for k in range(owners_here)
        ]
    )

    pre = lax.dot_general(
        inputs, w_first, (((0,), (0,)), ((), ())), preferred_element_type=jnp.float32
    )
    gate = jax.nn.sigmoid(pre)
    scores = jnp.dot(pre * gate, w_score, precision=lax.Precision.HIGHEST)
    error_term = jax.nn.sigmoid(scores) - label_part
    derivative = gate * (1.0 + pre * (1.0 - gate))
    back = (error_term[:, None] * w_score[None, :] * derivative).astype(jnp.bfloat16)
    local_grad = jnp.dot(inputs, back, preferred_element_type=jnp.float32)
    gradient = reduce_rows(local_grad, dom_size, rep_size)

    score_rows = scores.reshape(owners_here, per_owner)
    returned = jnp.stack(
        [lax.ppermute(score_rows[k], ("dom", "rep"), score_pairs(k)) for k in range(owners_here)]
    )
    own_scores = jnp.take(returned, sent_at, axis=0).reshape(per_dev)
    return (hop_out, own_scores, gradient)


def solution(mesh):
    placed = (
        P("rep", "dom"),
        P("dom", "rep", None, None),
        P("dom", None),
        P("dom", None),
        P("dom", None),
        P(("dom", "rep")),
        P(),
        P(),
    )
    return jax.shard_map(
        on_device,
        mesh=mesh,
        in_specs=placed,
        out_specs=(P("rep", "dom"), P(("dom", "rep")), P("rep", None)),
        check_vma=False,
    )
```

```python
import jax
import jax.numpy as jnp
from jax import lax
from jax.sharding import PartitionSpec as P


def hop_terms(source_rows, tile_piece, spread):
    product_terms = jnp.einsum(
        "fjc,jrc->jfr", source_rows, tile_piece.astype(jnp.float32), precision=lax.Precision.HIGHEST
    )
    return jnp.einsum("jb,jfr->fbr", spread, product_terms, precision=lax.Precision.HIGHEST)


def gather_all(values, axes, count):
    copies = jnp.broadcast_to(values[None], (count,) + values.shape)
    return lax.all_to_all(copies, axes, 0, 0, tiled=True).reshape((count * values.shape[0],) + values.shape[1:])


def halve_in_order(values, steps, bit_names, sizes):
    names = list(bit_names)
    values = values.reshape((2,) * len(names) + (values.shape[0] >> len(names),) + values.shape[1:])
    for name in steps:
        axis, bit_at = name
        position = names.index(name)
        bit = (lax.axis_index(axis) >> bit_at) & 1
        keep = lax.dynamic_index_in_dim(values, bit, position, keepdims=False)
        give = lax.dynamic_index_in_dim(values, 1 - bit, position, keepdims=False)
        pairs = [(i, i ^ (1 << bit_at)) for i in range(sizes[axis])]
        values = keep + lax.ppermute(give, axis, pairs)
        names.pop(position)
    return values


def reduce_rows(local_grad, dom_size, rep_size):
    rows, cols = local_grad.shape
    piece = rows // (rep_size * dom_size)
    if rep_size & (rep_size - 1) == 0 and dom_size & (dom_size - 1) == 0 and cols % 2 == 0:
        rep_bits = [("rep", b) for b in range(rep_size.bit_length() - 1)]
        dom_bits = [("dom", b) for b in range(dom_size.bit_length() - 1)]
        bit_names = rep_bits[::-1] + dom_bits[::-1]
        sizes = {"rep": rep_size, "dom": dom_size}
        first = halve_in_order(local_grad[:, : cols // 2], rep_bits + dom_bits, bit_names, sizes)
        second = halve_in_order(local_grad[:, cols // 2 :], rep_bits[:1] + dom_bits + rep_bits[1:], bit_names, sizes)
        parts = jnp.concatenate([first, second], axis=-1)
    else:
        parts = local_grad.reshape(rep_size, dom_size, piece, cols)
        parts = lax.all_to_all(parts, "rep", 0, 0, tiled=True).sum(0)
        parts = lax.all_to_all(parts, "dom", 0, 0, tiled=True).sum(0)
    return gather_all(parts, "dom", dom_size)


def on_device(features_t, tiles, send_block, tile_row, order, labels, w_first, w_score):
    feat_cols, row_count = features_t.shape
    tile_size = tiles.shape[-1]
    block_count = row_count // tile_size
    dom_size = lax.axis_size("dom")
    rep_size = lax.axis_size("rep")
    dom_at = lax.axis_index("dom")
    rep_at = lax.axis_index("rep")
    per_dev = labels.shape[0]
    per_owner = row_count // dom_size
    owners_here = per_dev // per_owner
    chunk_ids = jnp.arange(owners_here, dtype=jnp.int32)
    rotated = (chunk_ids + dom_at) % owners_here
    node_ids = order[0].reshape(rep_size, owners_here, per_owner)
    node_ids = jnp.take(node_ids, rotated, axis=1).reshape(row_count)
    select = (jnp.arange(row_count, dtype=jnp.int32)[:, None] == node_ids[None, :]).astype(jnp.bfloat16)

    def spread_samples(rows):
        picked = jnp.dot(rows.astype(jnp.bfloat16), select, preferred_element_type=jnp.float32).astype(jnp.bfloat16)
        return lax.all_to_all(picked, "rep", split_axis=1, concat_axis=0, tiled=True)

    plain_got = spread_samples(features_t)

    node_blocks = features_t.reshape(feat_cols, block_count, tile_size)
    outgoing = jnp.take(node_blocks, send_block[0], axis=1)
    block_ids = jnp.arange(block_count, dtype=jnp.int32)
    placed = (tile_row[0][:, None] == block_ids[None, :]).astype(jnp.float32)
    local_tiles = tiles[0]
    arrived = lax.all_to_all(outgoing, "dom", split_axis=1, concat_axis=1, tiled=True)
    hopped = hop_terms(arrived, lax.all_gather(local_tiles, "rep", axis=0, tiled=True), placed)
    hop_out = hopped.reshape(feat_cols, row_count)
    hop_got = spread_samples(hop_out)
    inputs = jnp.concatenate([plain_got, hop_got], axis=0)

    def score_pairs(k):
        pairs = []
        for j in range(dom_size):
            for r in range(rep_size):
                owner = (r * owners_here + (k + j) % owners_here) * rep_size + j // owners_here
                pairs.append((j * rep_size + r, owner))
        return pairs

    label_rows = labels.astype(jnp.float32).reshape(owners_here, per_owner)
    sent_at = (dom_at % owners_here - chunk_ids) % owners_here
    label_part = jnp.concatenate(
        [
            lax.ppermute(label_rows[sent_at[k]], ("dom", "rep"), [(b, a) for a, b in score_pairs(k)])
            for k in range(owners_here)
        ]
    )

    pre = lax.dot_general(
        inputs, w_first, (((0,), (0,)), ((), ())), preferred_element_type=jnp.float32
    )
    gate = jax.nn.sigmoid(pre)
    scores = jnp.dot(pre * gate, w_score, precision=lax.Precision.HIGHEST)
    error_term = jax.nn.sigmoid(scores) - label_part
    derivative = gate * (1.0 + pre * (1.0 - gate))
    back = (error_term[:, None] * w_score[None, :] * derivative).astype(jnp.bfloat16)
    local_grad = jnp.dot(inputs, back, preferred_element_type=jnp.float32)
    gradient = reduce_rows(local_grad, dom_size, rep_size)

    score_rows = scores.reshape(owners_here, per_owner)
    returned = jnp.stack(
        [lax.ppermute(score_rows[k], ("dom", "rep"), score_pairs(k)) for k in range(owners_here)]
    )
    own_scores = jnp.take(returned, sent_at, axis=0).reshape(per_dev)
    return (hop_out, own_scores, gradient)


def solution(mesh):
    placed = (
        P("rep", "dom"),
        P("dom", "rep", None, None),
        P("dom", None),
        P("dom", None),
        P("dom", None),
        P(("dom", "rep")),
        P(),
        P(),
    )
    return jax.shard_map(
        on_device,
        mesh=mesh,
        in_specs=placed,
        out_specs=(P("rep", "dom"), P(("dom", "rep")), P("rep", None)),
        check_vma=False,
    )
```

```python
import jax
import jax.numpy as jnp
from jax import lax
from jax.sharding import PartitionSpec as P


def hop_terms(source_rows, tile_piece, spread):
    product_terms = jnp.einsum(
        "fjc,jrc->jfr", source_rows, tile_piece.astype(jnp.float32), precision=lax.Precision.HIGHEST
    )
    return jnp.einsum("jb,jfr->fbr", spread, product_terms, precision=lax.Precision.HIGHEST)


def gather_all(values, axes, count):
    copies = jnp.broadcast_to(values[None], (count,) + values.shape)
    return lax.all_to_all(copies, axes, 0, 0, tiled=True).reshape((count * values.shape[0],) + values.shape[1:])


def gather_tiles(local_tiles, rep_at, rep_size):
    shifted = [local_tiles] + [
        lax.ppermute(local_tiles, "rep", [(i, (i + s) % rep_size) for i in range(rep_size)])
        for s in range(1, rep_size)
    ]
    from_shift = (rep_at - jnp.arange(rep_size, dtype=jnp.int32)) % rep_size
    return jnp.take(jnp.stack(shifted), from_shift, axis=0).reshape((-1,) + local_tiles.shape[1:])


def halve_in_order(values, steps, bit_names, sizes):
    names = list(bit_names)
    values = values.reshape((2,) * len(names) + (values.shape[0] >> len(names),) + values.shape[1:])
    for name in steps:
        axis, bit_at = name
        position = names.index(name)
        bit = (lax.axis_index(axis) >> bit_at) & 1
        keep = lax.dynamic_index_in_dim(values, bit, position, keepdims=False)
        give = lax.dynamic_index_in_dim(values, 1 - bit, position, keepdims=False)
        pairs = [(i, i ^ (1 << bit_at)) for i in range(sizes[axis])]
        values = keep + lax.ppermute(give, axis, pairs)
        names.pop(position)
    return values


def reduce_rows(local_grad, dom_size, rep_size):
    rows, cols = local_grad.shape
    piece = rows // (rep_size * dom_size)
    if rep_size & (rep_size - 1) == 0 and dom_size & (dom_size - 1) == 0 and cols % 2 == 0:
        rep_bits = [("rep", b) for b in range(rep_size.bit_length() - 1)]
        dom_bits = [("dom", b) for b in range(dom_size.bit_length() - 1)]
        bit_names = rep_bits[::-1] + dom_bits[::-1]
        sizes = {"rep": rep_size, "dom": dom_size}
        first = halve_in_order(local_grad[:, : cols // 2], rep_bits + dom_bits, bit_names, sizes)
        second = halve_in_order(local_grad[:, cols // 2 :], rep_bits[:1] + dom_bits + rep_bits[1:], bit_names, sizes)
        parts = jnp.concatenate([first, second], axis=-1)
    else:
        parts = local_grad.reshape(rep_size, dom_size, piece, cols)
        parts = lax.all_to_all(parts, "rep", 0, 0, tiled=True).sum(0)
        parts = lax.all_to_all(parts, "dom", 0, 0, tiled=True).sum(0)
    return gather_all(parts, "dom", dom_size)


def on_device(features_t, tiles, send_block, tile_row, order, labels, w_first, w_score):
    feat_cols, row_count = features_t.shape
    tile_size = tiles.shape[-1]
    block_count = row_count // tile_size
    dom_size = lax.axis_size("dom")
    rep_size = lax.axis_size("rep")
    dom_at = lax.axis_index("dom")
    rep_at = lax.axis_index("rep")
    outgoing = jnp.stack(
        [lax.dynamic_slice_in_dim(features_t, send_block[0, i] * tile_size, tile_size, 1) for i in range(dom_size)],
        axis=1,
    )
    block_ids = jnp.arange(block_count, dtype=jnp.int32)
    placed = (tile_row[0][:, None] == block_ids[None, :]).astype(jnp.float32)
    local_tiles = tiles[0]
    arrived = lax.all_to_all(outgoing, "dom", split_axis=1, concat_axis=1, tiled=True)
    hopped = hop_terms(arrived, gather_tiles(local_tiles, rep_at, rep_size), placed)
    hop_out = hopped.reshape(feat_cols, row_count)

    per_dev = labels.shape[0]
    per_owner = row_count // dom_size
    owners_here = per_dev // per_owner
    chunk_ids = jnp.arange(owners_here, dtype=jnp.int32)
    rotated = (chunk_ids + dom_at) % owners_here
    node_ids = order[0].reshape(rep_size, owners_here, per_owner)
    node_ids = jnp.take(node_ids, rotated, axis=1).reshape(row_count)
    rows_here = jnp.concatenate([features_t.astype(jnp.bfloat16), hop_out.astype(jnp.bfloat16)], axis=0)
    select = (jnp.arange(row_count, dtype=jnp.int32)[:, None] == node_ids[None, :]).astype(jnp.bfloat16)
    picked = jnp.dot(rows_here, select, preferred_element_type=jnp.float32).astype(jnp.bfloat16)
    got = lax.all_to_all(picked, "rep", split_axis=1, concat_axis=0, tiled=True)
    inputs = got.reshape(rep_size, 2, feat_cols, per_dev).transpose(1, 0, 2, 3).reshape(-1, per_dev)

    def score_pairs(k):
        pairs = []
        for j in range(dom_size):
            for r in range(rep_size):
                owner = (r * owners_here + (k + j) % owners_here) * rep_size + j // owners_here
                pairs.append((j * rep_size + r, owner))
        return pairs

    label_rows = labels.astype(jnp.float32).reshape(owners_here, per_owner)
    sent_at = (dom_at % owners_here - chunk_ids) % owners_here
    label_part = jnp.concatenate(
        [
            lax.ppermute(label_rows[sent_at[k]], ("dom", "rep"), [(b, a) for a, b in score_pairs(k)])
            for k in range(owners_here)
        ]
    )

    pre = lax.dot_general(
        inputs, w_first, (((0,), (0,)), ((), ())), preferred_element_type=jnp.float32
    )
    gate = jax.nn.sigmoid(pre)
    scores = jnp.dot(pre * gate, w_score, precision=lax.Precision.HIGHEST)
    error_term = jax.nn.sigmoid(scores) - label_part
    derivative = gate * (1.0 + pre * (1.0 - gate))
    back = (error_term[:, None] * w_score[None, :] * derivative).astype(jnp.bfloat16)
    local_grad = jnp.dot(inputs, back, preferred_element_type=jnp.float32)
    gradient = reduce_rows(local_grad, dom_size, rep_size)

    score_rows = scores.reshape(owners_here, per_owner)
    returned = jnp.stack(
        [lax.ppermute(score_rows[k], ("dom", "rep"), score_pairs(k)) for k in range(owners_here)]
    )
    own_scores = jnp.take(returned, sent_at, axis=0).reshape(per_dev)
    return (hop_out, own_scores, gradient)


def solution(mesh):
    placed = (
        P("rep", "dom"),
        P("dom", "rep", None, None),
        P("dom", None),
        P("dom", None),
        P("dom", None),
        P(("dom", "rep")),
        P(),
        P(),
    )
    return jax.shard_map(
        on_device,
        mesh=mesh,
        in_specs=placed,
        out_specs=(P("rep", "dom"), P(("dom", "rep")), P("rep", None)),
        check_vma=False,
    )
```

```python
import jax
import jax.numpy as jnp
from jax import lax
from jax.sharding import PartitionSpec as P


def hop_terms(source_rows, tile_piece, spread):
    product_terms = jnp.einsum(
        "fjc,jrc->jfr", source_rows, tile_piece.astype(jnp.float32), precision=lax.Precision.HIGHEST
    )
    return jnp.einsum("jb,jfr->fbr", spread, product_terms, precision=lax.Precision.HIGHEST)


def gather_all(values, axes, count):
    copies = jnp.broadcast_to(values[None], (count,) + values.shape)
    return lax.all_to_all(copies, axes, 0, 0, tiled=True).reshape((count * values.shape[0],) + values.shape[1:])


def halve_in_order(values, steps, bit_names, sizes):
    names = list(bit_names)
    values = values.reshape((2,) * len(names) + (values.shape[0] >> len(names),) + values.shape[1:])
    for name in steps:
        axis, bit_at = name
        position = names.index(name)
        bit = (lax.axis_index(axis) >> bit_at) & 1
        keep = lax.dynamic_index_in_dim(values, bit, position, keepdims=False)
        give = lax.dynamic_index_in_dim(values, 1 - bit, position, keepdims=False)
        pairs = [(i, i ^ (1 << bit_at)) for i in range(sizes[axis])]
        values = keep + lax.ppermute(give, axis, pairs)
        names.pop(position)
    return values


def reduce_rows(inputs, back, dom_size, rep_size):
    rows, cols = inputs.shape[0], back.shape[1]
    piece = rows // (rep_size * dom_size)
    if rep_size & (rep_size - 1) == 0 and dom_size & (dom_size - 1) == 0 and rep_size > 1 and cols % 2 == 0:
        rep_bits = [("rep", b) for b in range(rep_size.bit_length() - 1)]
        dom_bits = [("dom", b) for b in range(dom_size.bit_length() - 1)]
        sizes = {"rep": rep_size, "dom": dom_size}
        bit = lax.axis_index("rep") & 1
        halves = inputs.reshape(rows // (2 * piece * dom_size), 2, -1)
        kept_rows = lax.dynamic_index_in_dim(halves, bit, 1, keepdims=False).reshape(rows // 2, -1)
        given_rows = lax.dynamic_index_in_dim(halves, 1 - bit, 1, keepdims=False).reshape(rows // 2, -1)
        keep = jnp.dot(kept_rows, back, preferred_element_type=jnp.float32)
        give = jnp.dot(given_rows, back, preferred_element_type=jnp.float32)
        summed = keep + lax.ppermute(give, "rep", [(i, i ^ 1) for i in range(rep_size)])
        bit_names = rep_bits[:0:-1] + dom_bits[::-1]
        first = halve_in_order(summed[:, : cols // 2], rep_bits[1:] + dom_bits, bit_names, sizes)
        second = halve_in_order(summed[:, cols // 2 :], dom_bits + rep_bits[1:], bit_names, sizes)
        parts = jnp.concatenate([first, second], axis=-1)
    else:
        local_grad = jnp.dot(inputs, back, preferred_element_type=jnp.float32)
        parts = local_grad.reshape(rep_size, dom_size, piece, cols)
        parts = lax.all_to_all(parts, "rep", 0, 0, tiled=True).sum(0)
        parts = lax.all_to_all(parts, "dom", 0, 0, tiled=True).sum(0)
    return gather_all(parts, "dom", dom_size)


def on_device(features_t, tiles, send_block, tile_row, order, labels, w_first, w_score):
    feat_cols, row_count = features_t.shape
    tile_size = tiles.shape[-1]
    block_count = row_count // tile_size
    dom_size = lax.axis_size("dom")
    rep_size = lax.axis_size("rep")
    dom_at = lax.axis_index("dom")
    rep_at = lax.axis_index("rep")
    node_blocks = features_t.reshape(feat_cols, block_count, tile_size)
    outgoing = jnp.take(node_blocks, send_block[0], axis=1)
    block_ids = jnp.arange(block_count, dtype=jnp.int32)
    placed = (tile_row[0][:, None] == block_ids[None, :]).astype(jnp.float32)
    local_tiles = tiles[0]
    arrived = lax.all_to_all(outgoing, "dom", split_axis=1, concat_axis=1, tiled=True)
    hopped = hop_terms(arrived, lax.all_gather(local_tiles, "rep", axis=0, tiled=True), placed)
    hop_out = hopped.reshape(feat_cols, row_count)

    per_dev = labels.shape[0]
    per_owner = row_count // dom_size
    owners_here = per_dev // per_owner
    chunk_ids = jnp.arange(owners_here, dtype=jnp.int32)
    rotated = (chunk_ids + dom_at) % owners_here
    node_ids = order[0].reshape(rep_size, owners_here, per_owner)
    node_ids = jnp.take(node_ids, rotated, axis=1).reshape(row_count)
    rows_here = jnp.concatenate([features_t.astype(jnp.bfloat16), hop_out.astype(jnp.bfloat16)], axis=0)
    select = (jnp.arange(row_count, dtype=jnp.int32)[:, None] == node_ids[None, :]).astype(jnp.bfloat16)
    picked = jnp.dot(rows_here, select, preferred_element_type=jnp.float32).astype(jnp.bfloat16)
    got = lax.all_to_all(picked, "rep", split_axis=1, concat_axis=0, tiled=True)
    inputs = got.reshape(rep_size, 2, feat_cols, per_dev).transpose(1, 0, 2, 3).reshape(-1, per_dev)

    def score_pairs(k):
        pairs = []
        for j in range(dom_size):
            for r in range(rep_size):
                owner = (r * owners_here + (k + j) % owners_here) * rep_size + j // owners_here
                pairs.append((j * rep_size + r, owner))
        return pairs

    label_rows = labels.astype(jnp.float32).reshape(owners_here, per_owner)
    sent_at = (dom_at % owners_here - chunk_ids) % owners_here
    label_part = jnp.concatenate(
        [
            lax.ppermute(label_rows[sent_at[k]], ("dom", "rep"), [(b, a) for a, b in score_pairs(k)])
            for k in range(owners_here)
        ]
    )

    pre = lax.dot_general(
        inputs, w_first, (((0,), (0,)), ((), ())), preferred_element_type=jnp.float32
    )
    gate = jax.nn.sigmoid(pre)
    scores = jnp.dot(pre * gate, w_score, precision=lax.Precision.HIGHEST)
    error_term = jax.nn.sigmoid(scores) - label_part
    derivative = gate * (1.0 + pre * (1.0 - gate))
    back = (error_term[:, None] * w_score[None, :] * derivative).astype(jnp.bfloat16)
    gradient = reduce_rows(inputs, back, dom_size, rep_size)

    score_rows = scores.reshape(owners_here, per_owner)
    returned = jnp.stack(
        [lax.ppermute(score_rows[k], ("dom", "rep"), score_pairs(k)) for k in range(owners_here)]
    )
    own_scores = jnp.take(returned, sent_at, axis=0).reshape(per_dev)
    return (hop_out, own_scores, gradient)


def solution(mesh):
    placed = (
        P("rep", "dom"),
        P("dom", "rep", None, None),
        P("dom", None),
        P("dom", None),
        P("dom", None),
        P(("dom", "rep")),
        P(),
        P(),
    )
    return jax.shard_map(
        on_device,
        mesh=mesh,
        in_specs=placed,
        out_specs=(P("rep", "dom"), P(("dom", "rep")), P("rep", None)),
        check_vma=False,
    )
```

```python
import jax
import jax.numpy as jnp
from jax import lax
from jax.sharding import PartitionSpec as P


def hop_terms(source_rows, tile_piece, spread):
    product_terms = jnp.einsum(
        "fjc,jrc->jfr", source_rows, tile_piece.astype(jnp.float32), precision=lax.Precision.HIGHEST
    )
    return jnp.einsum("jb,jfr->fbr", spread, product_terms, precision=lax.Precision.HIGHEST)


def gather_all(values, axes, count):
    copies = jnp.broadcast_to(values[None], (count,) + values.shape)
    return lax.all_to_all(copies, axes, 0, 0, tiled=True).reshape((count * values.shape[0],) + values.shape[1:])


def halve_in_order(values, steps, bit_names, sizes):
    names = list(bit_names)
    values = values.reshape((2,) * len(names) + (values.shape[0] >> len(names),) + values.shape[1:])
    for name in steps:
        axis, bit_at = name
        position = names.index(name)
        bit = (lax.axis_index(axis) >> bit_at) & 1
        keep = lax.dynamic_index_in_dim(values, bit, position, keepdims=False)
        give = lax.dynamic_index_in_dim(values, 1 - bit, position, keepdims=False)
        pairs = [(i, i ^ (1 << bit_at)) for i in range(sizes[axis])]
        values = keep + lax.ppermute(give, axis, pairs)
        names.pop(position)
    return values


def reduce_rows(local_grad, dom_size, rep_size):
    rows, cols = local_grad.shape
    piece = rows // (rep_size * dom_size)
    if rep_size & (rep_size - 1) == 0 and dom_size & (dom_size - 1) == 0 and cols % 2 == 0:
        rep_bits = [("rep", b) for b in range(rep_size.bit_length() - 1)]
        dom_bits = [("dom", b) for b in range(dom_size.bit_length() - 1)]
        bit_names = rep_bits[::-1] + dom_bits[::-1]
        sizes = {"rep": rep_size, "dom": dom_size}
        first = halve_in_order(local_grad[:, : cols // 2], rep_bits + dom_bits, bit_names, sizes)
        second = halve_in_order(local_grad[:, cols // 2 :], rep_bits[:1] + dom_bits + rep_bits[1:], bit_names, sizes)
        parts = jnp.concatenate([first, second], axis=-1)
    else:
        parts = local_grad.reshape(rep_size, dom_size, piece, cols)
        parts = lax.all_to_all(parts, "rep", 0, 0, tiled=True).sum(0)
        parts = lax.all_to_all(parts, "dom", 0, 0, tiled=True).sum(0)
    return gather_all(parts, "dom", dom_size)


def on_device(features_t, tiles, send_block, tile_row, order, labels, w_first, w_score):
    feat_cols, row_count = features_t.shape
    tile_size = tiles.shape[-1]
    block_count = row_count // tile_size
    dom_size = lax.axis_size("dom")
    rep_size = lax.axis_size("rep")
    dom_at = lax.axis_index("dom")
    rep_at = lax.axis_index("rep")
    node_blocks = features_t.reshape(feat_cols, block_count, tile_size)
    block_ids = jnp.arange(block_count, dtype=jnp.int32)
    sent = (send_block[0][:, None] == block_ids[None, :]).astype(jnp.float32)
    outgoing = jnp.einsum("fbc,jb->fjc", node_blocks, sent, precision=lax.Precision.HIGHEST)
    placed = (tile_row[0][:, None] == block_ids[None, :]).astype(jnp.float32)
    local_tiles = tiles[0]
    arrived = lax.all_to_all(outgoing, "dom", split_axis=1, concat_axis=1, tiled=True)
    hopped = hop_terms(arrived, lax.all_gather(local_tiles, "rep", axis=0, tiled=True), placed)
    hop_out = hopped.reshape(feat_cols, row_count)

    per_dev = labels.shape[0]
    per_owner = row_count // dom_size
    owners_here = per_dev // per_owner
    chunk_ids = jnp.arange(owners_here, dtype=jnp.int32)
    rotated = (chunk_ids + dom_at) % owners_here
    node_ids = order[0].reshape(rep_size, owners_here, per_owner)
    node_ids = jnp.take(node_ids, rotated, axis=1).reshape(row_count)
    rows_here = jnp.concatenate([features_t.astype(jnp.bfloat16), hop_out.astype(jnp.bfloat16)], axis=0)
    select = (jnp.arange(row_count, dtype=jnp.int32)[:, None] == node_ids[None, :]).astype(jnp.bfloat16)
    picked = jnp.dot(rows_here, select, preferred_element_type=jnp.float32).astype(jnp.bfloat16)
    got = lax.all_to_all(picked, "rep", split_axis=1, concat_axis=0, tiled=True)
    inputs = got.reshape(rep_size, 2, feat_cols, per_dev).transpose(1, 0, 2, 3).reshape(-1, per_dev)

    def score_pairs(k):
        pairs = []
        for j in range(dom_size):
            for r in range(rep_size):
                owner = (r * owners_here + (k + j) % owners_here) * rep_size + j // owners_here
                pairs.append((j * rep_size + r, owner))
        return pairs

    label_rows = labels.astype(jnp.float32).reshape(owners_here, per_owner)
    sent_at = (dom_at % owners_here - chunk_ids) % owners_here
    label_part = jnp.concatenate(
        [
            lax.ppermute(label_rows[sent_at[k]], ("dom", "rep"), [(b, a) for a, b in score_pairs(k)])
            for k in range(owners_here)
        ]
    )

    pre = lax.dot_general(
        inputs, w_first, (((0,), (0,)), ((), ())), preferred_element_type=jnp.float32
    )
    gate = jax.nn.sigmoid(pre)
    scores = jnp.dot(pre * gate, w_score, precision=lax.Precision.HIGHEST)
    error_term = jax.nn.sigmoid(scores) - label_part
    derivative = gate * (1.0 + pre * (1.0 - gate))
    back = (error_term[:, None] * w_score[None, :] * derivative).astype(jnp.bfloat16)
    local_grad = jnp.dot(inputs, back, preferred_element_type=jnp.float32)
    gradient = reduce_rows(local_grad, dom_size, rep_size)

    score_rows = scores.reshape(owners_here, per_owner)
    returned = jnp.stack(
        [lax.ppermute(score_rows[k], ("dom", "rep"), score_pairs(k)) for k in range(owners_here)]
    )
    own_scores = jnp.take(returned, sent_at, axis=0).reshape(per_dev)
    return (hop_out, own_scores, gradient)


def solution(mesh):
    placed = (
        P("rep", "dom"),
        P("dom", "rep", None, None),
        P("dom", None),
        P("dom", None),
        P("dom", None),
        P(("dom", "rep")),
        P(),
        P(),
    )
    return jax.shard_map(
        on_device,
        mesh=mesh,
        in_specs=placed,
        out_specs=(P("rep", "dom"), P(("dom", "rep")), P("rep", None)),
        check_vma=False,
    )
```

```python
import jax
import jax.numpy as jnp
from jax import lax
from jax.sharding import PartitionSpec as P


def hop_terms(source_rows, tile_piece, spread):
    product_terms = jnp.einsum(
        "fjc,jrc->jfr", source_rows, tile_piece.astype(jnp.float32), precision=lax.Precision.HIGHEST
    )
    return jnp.einsum("jb,jfr->fbr", spread, product_terms, precision=lax.Precision.HIGHEST)


def gather_all(values, axes, count):
    copies = jnp.broadcast_to(values[None], (count,) + values.shape)
    return lax.all_to_all(copies, axes, 0, 0, tiled=True).reshape((count * values.shape[0],) + values.shape[1:])


def halve_in_order(values, steps, bit_names, sizes):
    names = list(bit_names)
    values = values.reshape((2,) * len(names) + (values.shape[0] >> len(names),) + values.shape[1:])
    for name in steps:
        axis, bit_at = name
        position = names.index(name)
        bit = (lax.axis_index(axis) >> bit_at) & 1
        keep = lax.dynamic_index_in_dim(values, bit, position, keepdims=False)
        give = lax.dynamic_index_in_dim(values, 1 - bit, position, keepdims=False)
        pairs = [(i, i ^ (1 << bit_at)) for i in range(sizes[axis])]
        values = keep + lax.ppermute(give, axis, pairs)
        names.pop(position)
    return values


def reduce_rows(local_grad, extra, dom_size, rep_size):
    rows, cols = local_grad.shape
    piece = rows // (rep_size * dom_size)
    if rep_size & (rep_size - 1) == 0 and dom_size & (dom_size - 1) == 0 and cols % 2 == 0:
        rep_bits = [("rep", b) for b in range(rep_size.bit_length() - 1)]
        dom_bits = [("dom", b) for b in range(dom_size.bit_length() - 1)]
        bit_names = rep_bits[::-1] + dom_bits[::-1]
        sizes = {"rep": rep_size, "dom": dom_size}
        first = halve_in_order(local_grad[:, : cols // 2], rep_bits + dom_bits, bit_names, sizes)
        second_in = jnp.concatenate([local_grad[:, cols // 2 :], extra], axis=-1)
        second = halve_in_order(second_in, rep_bits[:1] + dom_bits + rep_bits[1:], bit_names, sizes)
        parts = jnp.concatenate([first, second[:, : cols - cols // 2]], axis=-1)
        own_extra = second[:, cols - cols // 2 :]
    else:
        both = jnp.concatenate([local_grad, extra], axis=-1)
        both = both.reshape(rep_size, dom_size, piece, -1)
        both = lax.all_to_all(both, "rep", 0, 0, tiled=True).sum(0)
        both = lax.all_to_all(both, "dom", 0, 0, tiled=True).sum(0)
        parts, own_extra = both[:, :cols], both[:, cols:]
    return gather_all(parts, "dom", dom_size), own_extra


def on_device(features_t, tiles, send_block, tile_row, order, labels, w_first, w_score):
    feat_cols, row_count = features_t.shape
    tile_size = tiles.shape[-1]
    block_count = row_count // tile_size
    dom_size = lax.axis_size("dom")
    rep_size = lax.axis_size("rep")
    dom_at = lax.axis_index("dom")
    rep_at = lax.axis_index("rep")
    node_blocks = features_t.reshape(feat_cols, block_count, tile_size)
    block_ids = jnp.arange(block_count, dtype=jnp.int32)
    sent = (send_block[0][:, None] == block_ids[None, :]).astype(jnp.float32)
    outgoing = jnp.einsum("fbc,jb->fjc", node_blocks, sent, precision=lax.Precision.HIGHEST)
    placed = (tile_row[0][:, None] == block_ids[None, :]).astype(jnp.float32)
    local_tiles = tiles[0]
    arrived = lax.all_to_all(outgoing, "dom", split_axis=1, concat_axis=1, tiled=True)
    hopped = hop_terms(arrived, lax.all_gather(local_tiles, "rep", axis=0, tiled=True), placed)
    hop_out = hopped.reshape(feat_cols, row_count)

    per_dev = labels.shape[0]
    per_owner = row_count // dom_size
    owners_here = per_dev // per_owner
    chunk_ids = jnp.arange(owners_here, dtype=jnp.int32)
    rotated = (chunk_ids + dom_at) % owners_here
    node_ids = order[0].reshape(rep_size, owners_here, per_owner)
    node_ids = jnp.take(node_ids, rotated, axis=1).reshape(row_count)
    rows_here = jnp.concatenate([features_t.astype(jnp.bfloat16), hop_out.astype(jnp.bfloat16)], axis=0)
    select = (jnp.arange(row_count, dtype=jnp.int32)[:, None] == node_ids[None, :]).astype(jnp.bfloat16)
    picked = jnp.dot(rows_here, select, preferred_element_type=jnp.float32).astype(jnp.bfloat16)
    got = lax.all_to_all(picked, "rep", split_axis=1, concat_axis=0, tiled=True)
    inputs = got.reshape(rep_size, 2, feat_cols, per_dev).transpose(1, 0, 2, 3).reshape(-1, per_dev)

    def score_pairs(k):
        pairs = []
        for j in range(dom_size):
            for r in range(rep_size):
                owner = (r * owners_here + (k + j) % owners_here) * rep_size + j // owners_here
                pairs.append((j * rep_size + r, owner))
        return pairs

    label_rows = labels.astype(jnp.float32).reshape(owners_here, per_owner)
    sent_at = (dom_at % owners_here - chunk_ids) % owners_here
    label_part = jnp.concatenate(
        [
            lax.ppermute(label_rows[sent_at[k]], ("dom", "rep"), [(b, a) for a, b in score_pairs(k)])
            for k in range(owners_here)
        ]
    )

    pre = lax.dot_general(
        inputs, w_first, (((0,), (0,)), ((), ())), preferred_element_type=jnp.float32
    )
    gate = jax.nn.sigmoid(pre)
    scores = jnp.dot(pre * gate, w_score, precision=lax.Precision.HIGHEST)
    error_term = jax.nn.sigmoid(scores) - label_part
    derivative = gate * (1.0 + pre * (1.0 - gate))
    back = (error_term[:, None] * w_score[None, :] * derivative).astype(jnp.bfloat16)
    local_grad = jnp.dot(inputs, back, preferred_element_type=jnp.float32)
    grid = jnp.zeros((rep_size, dom_size, per_dev), jnp.float32)
    for k in range(owners_here):
        owner_dom = rep_at * owners_here + (k + dom_at) % owners_here
        grid = lax.dynamic_update_slice(
            grid,
            scores[k * per_owner : (k + 1) * per_owner].reshape(1, 1, per_owner),
            (dom_at // owners_here, owner_dom, (dom_at % owners_here) * per_owner),
        )
    piece = local_grad.shape[0] // (rep_size * dom_size)
    gradient, own_scores = reduce_rows(
        local_grad, grid.reshape(local_grad.shape[0], per_dev // piece), dom_size, rep_size
    )
    own_scores = own_scores.reshape(per_dev)

    return (hop_out, own_scores, gradient)


def solution(mesh):
    placed = (
        P("rep", "dom"),
        P("dom", "rep", None, None),
        P("dom", None),
        P("dom", None),
        P("dom", None),
        P(("dom", "rep")),
        P(),
        P(),
    )
    return jax.shard_map(
        on_device,
        mesh=mesh,
        in_specs=placed,
        out_specs=(P("rep", "dom"), P(("dom", "rep")), P("rep", None)),
        check_vma=False,
    )
```

```python
import jax
import jax.numpy as jnp
from jax import lax
from jax.sharding import PartitionSpec as P


def hop_terms(source_rows, tile_piece, spread):
    product_terms = jnp.einsum(
        "fjc,jrc->jfr", source_rows, tile_piece.astype(jnp.float32), precision=lax.Precision.HIGHEST
    )
    return jnp.einsum("jb,jfr->fbr", spread, product_terms, precision=lax.Precision.HIGHEST)


def gather_all(values, axes, count):
    copies = jnp.broadcast_to(values[None], (count,) + values.shape)
    return lax.all_to_all(copies, axes, 0, 0, tiled=True).reshape((count * values.shape[0],) + values.shape[1:])


def halve_in_order(values, steps, bit_names, sizes):
    names = list(bit_names)
    values = values.reshape((2,) * len(names) + (values.shape[0] >> len(names),) + values.shape[1:])
    for name in steps:
        axis, bit_at = name
        position = names.index(name)
        bit = (lax.axis_index(axis) >> bit_at) & 1
        keep = lax.dynamic_index_in_dim(values, bit, position, keepdims=False)
        give = lax.dynamic_index_in_dim(values, 1 - bit, position, keepdims=False)
        pairs = [(i, i ^ (1 << bit_at)) for i in range(sizes[axis])]
        values = keep + lax.ppermute(give, axis, pairs)
        names.pop(position)
    return values


def reduce_rows(local_grad, dom_size, rep_size):
    rows, cols = local_grad.shape
    piece = rows // (rep_size * dom_size)
    if rep_size & (rep_size - 1) == 0 and dom_size & (dom_size - 1) == 0 and cols % 2 == 0:
        rep_bits = [("rep", b) for b in range(rep_size.bit_length() - 1)]
        dom_bits = [("dom", b) for b in range(dom_size.bit_length() - 1)]
        bit_names = rep_bits[::-1] + dom_bits[::-1]
        sizes = {"rep": rep_size, "dom": dom_size}
        first = halve_in_order(local_grad[:, : cols // 2], rep_bits + dom_bits, bit_names, sizes)
        second = halve_in_order(local_grad[:, cols // 2 :], rep_bits[:1] + dom_bits + rep_bits[1:], bit_names, sizes)
        parts = jnp.concatenate([first, second], axis=-1)
    else:
        parts = local_grad.reshape(rep_size, dom_size, piece, cols)
        parts = lax.all_to_all(parts, "rep", 0, 0, tiled=True).sum(0)
        parts = lax.all_to_all(parts, "dom", 0, 0, tiled=True).sum(0)
    return gather_all(parts, "dom", dom_size)


def on_device(features_t, tiles, send_block, tile_row, order, labels, w_first, w_score):
    feat_cols, row_count = features_t.shape
    tile_size = tiles.shape[-1]
    block_count = row_count // tile_size
    dom_size = lax.axis_size("dom")
    rep_size = lax.axis_size("rep")
    dom_at = lax.axis_index("dom")
    rep_at = lax.axis_index("rep")
    per_dev = labels.shape[0]
    per_owner = row_count // dom_size
    owners_here = per_dev // per_owner
    chunk_ids = jnp.arange(owners_here, dtype=jnp.int32)

    def score_pairs(k):
        pairs = []
        for j in range(dom_size):
            for r in range(rep_size):
                owner = (r * owners_here + (k + j) % owners_here) * rep_size + j // owners_here
                pairs.append((j * rep_size + r, owner))
        return pairs

    label_rows = labels.astype(jnp.float32).reshape(owners_here, per_owner)
    sent_at = (dom_at % owners_here - chunk_ids) % owners_here
    label_part = jnp.concatenate(
        [
            lax.ppermute(label_rows[sent_at[k]], ("dom", "rep"), [(b, a) for a, b in score_pairs(k)])
            for k in range(owners_here)
        ]
    )

    node_blocks = features_t.reshape(feat_cols, block_count, tile_size)
    block_ids = jnp.arange(block_count, dtype=jnp.int32)
    sent = (send_block[0][:, None] == block_ids[None, :]).astype(jnp.float32)
    outgoing = jnp.einsum("fbc,jb->fjc", node_blocks, sent, precision=lax.Precision.HIGHEST)
    placed = (tile_row[0][:, None] == block_ids[None, :]).astype(jnp.float32)
    local_tiles = tiles[0]
    label_part, outgoing = lax.optimization_barrier((label_part, outgoing))
    arrived = lax.all_to_all(outgoing, "dom", split_axis=1, concat_axis=1, tiled=True)
    hopped = hop_terms(arrived, lax.all_gather(local_tiles, "rep", axis=0, tiled=True), placed)
    hop_out = hopped.reshape(feat_cols, row_count)

    rotated = (chunk_ids + dom_at) % owners_here
    node_ids = order[0].reshape(rep_size, owners_here, per_owner)
    node_ids = jnp.take(node_ids, rotated, axis=1).reshape(row_count)
    rows_here = jnp.concatenate([features_t.astype(jnp.bfloat16), hop_out.astype(jnp.bfloat16)], axis=0)
    select = (jnp.arange(row_count, dtype=jnp.int32)[:, None] == node_ids[None, :]).astype(jnp.bfloat16)
    picked = jnp.dot(rows_here, select, preferred_element_type=jnp.float32).astype(jnp.bfloat16)
    got = lax.all_to_all(picked, "rep", split_axis=1, concat_axis=0, tiled=True)
    inputs = got.reshape(rep_size, 2, feat_cols, per_dev).transpose(1, 0, 2, 3).reshape(-1, per_dev)

    pre = lax.dot_general(
        inputs, w_first, (((0,), (0,)), ((), ())), preferred_element_type=jnp.float32
    )
    gate = jax.nn.sigmoid(pre)
    scores = jnp.dot(pre * gate, w_score, precision=lax.Precision.HIGHEST)
    error_term = jax.nn.sigmoid(scores) - label_part
    derivative = gate * (1.0 + pre * (1.0 - gate))
    back = (error_term[:, None] * w_score[None, :] * derivative).astype(jnp.bfloat16)
    local_grad = jnp.dot(inputs, back, preferred_element_type=jnp.float32)
    gradient = reduce_rows(local_grad, dom_size, rep_size)

    score_rows = scores.reshape(owners_here, per_owner)
    returned = jnp.stack(
        [lax.ppermute(score_rows[k], ("dom", "rep"), score_pairs(k)) for k in range(owners_here)]
    )
    own_scores = jnp.take(returned, sent_at, axis=0).reshape(per_dev)
    return (hop_out, own_scores, gradient)


def solution(mesh):
    placed = (
        P("rep", "dom"),
        P("dom", "rep", None, None),
        P("dom", None),
        P("dom", None),
        P("dom", None),
        P(("dom", "rep")),
        P(),
        P(),
    )
    return jax.shard_map(
        on_device,
        mesh=mesh,
        in_specs=placed,
        out_specs=(P("rep", "dom"), P(("dom", "rep")), P("rep", None)),
        check_vma=False,
    )
```

```python
import jax
import jax.numpy as jnp
from jax import lax
from jax.sharding import PartitionSpec as P


def hop_terms(source_rows, tile_piece, spread):
    product_terms = jnp.einsum(
        "jfc,jrc->jfr", source_rows, tile_piece.astype(jnp.float32), precision=lax.Precision.HIGHEST
    )
    return jnp.einsum("jb,jfr->fbr", spread, product_terms, precision=lax.Precision.HIGHEST)


def gather_all(values, axes, count):
    copies = jnp.broadcast_to(values[None], (count,) + values.shape)
    return lax.all_to_all(copies, axes, 0, 0, tiled=True).reshape((count * values.shape[0],) + values.shape[1:])


def halve_in_order(values, steps, bit_names, sizes):
    names = list(bit_names)
    values = values.reshape((2,) * len(names) + (values.shape[0] >> len(names),) + values.shape[1:])
    for name in steps:
        axis, bit_at = name
        position = names.index(name)
        bit = (lax.axis_index(axis) >> bit_at) & 1
        keep = lax.dynamic_index_in_dim(values, bit, position, keepdims=False)
        give = lax.dynamic_index_in_dim(values, 1 - bit, position, keepdims=False)
        pairs = [(i, i ^ (1 << bit_at)) for i in range(sizes[axis])]
        values = keep + lax.ppermute(give, axis, pairs)
        names.pop(position)
    return values


def reduce_rows(local_grad, dom_size, rep_size):
    rows, cols = local_grad.shape
    piece = rows // (rep_size * dom_size)
    if rep_size & (rep_size - 1) == 0 and dom_size & (dom_size - 1) == 0 and cols % 2 == 0:
        rep_bits = [("rep", b) for b in range(rep_size.bit_length() - 1)]
        dom_bits = [("dom", b) for b in range(dom_size.bit_length() - 1)]
        bit_names = rep_bits[::-1] + dom_bits[::-1]
        sizes = {"rep": rep_size, "dom": dom_size}
        first = halve_in_order(local_grad[:, : cols // 2], rep_bits + dom_bits, bit_names, sizes)
        second = halve_in_order(local_grad[:, cols // 2 :], rep_bits[:1] + dom_bits + rep_bits[1:], bit_names, sizes)
        parts = jnp.concatenate([first, second], axis=-1)
    else:
        parts = local_grad.reshape(rep_size, dom_size, piece, cols)
        parts = lax.all_to_all(parts, "rep", 0, 0, tiled=True).sum(0)
        parts = lax.all_to_all(parts, "dom", 0, 0, tiled=True).sum(0)
    return gather_all(parts, "dom", dom_size)


def on_device(features_t, tiles, send_block, tile_row, order, labels, w_first, w_score):
    feat_cols, row_count = features_t.shape
    tile_size = tiles.shape[-1]
    block_count = row_count // tile_size
    dom_size = lax.axis_size("dom")
    rep_size = lax.axis_size("rep")
    dom_at = lax.axis_index("dom")
    rep_at = lax.axis_index("rep")
    node_blocks = features_t.reshape(feat_cols, block_count, tile_size)
    block_ids = jnp.arange(block_count, dtype=jnp.int32)
    sent = (send_block[0][:, None] == block_ids[None, :]).astype(jnp.float32)
    outgoing = jnp.einsum("fbc,jb->jfc", node_blocks, sent, precision=lax.Precision.HIGHEST)
    placed = (tile_row[0][:, None] == block_ids[None, :]).astype(jnp.float32)
    local_tiles = tiles[0]
    arrived = lax.all_to_all(outgoing, "dom", split_axis=0, concat_axis=0, tiled=True)
    hopped = hop_terms(arrived, lax.all_gather(local_tiles, "rep", axis=0, tiled=True), placed)
    hop_out = hopped.reshape(feat_cols, row_count)

    per_dev = labels.shape[0]
    per_owner = row_count // dom_size
    owners_here = per_dev // per_owner
    chunk_ids = jnp.arange(owners_here, dtype=jnp.int32)
    rotated = (chunk_ids + dom_at) % owners_here
    node_ids = order[0].reshape(rep_size, owners_here, per_owner)
    node_ids = jnp.take(node_ids, rotated, axis=1).reshape(row_count)
    rows_here = jnp.concatenate([features_t.astype(jnp.bfloat16), hop_out.astype(jnp.bfloat16)], axis=0)
    select = (jnp.arange(row_count, dtype=jnp.int32)[:, None] == node_ids[None, :]).astype(jnp.bfloat16)
    picked = jnp.einsum(
        "fn,nrq->rfq", rows_here, select.reshape(row_count, rep_size, per_dev), preferred_element_type=jnp.float32
    ).astype(jnp.bfloat16)
    got = lax.all_to_all(picked, "rep", split_axis=0, concat_axis=0, tiled=True)
    inputs = got.reshape(rep_size, 2, feat_cols, per_dev).transpose(1, 0, 2, 3).reshape(-1, per_dev)

    def score_pairs(k):
        pairs = []
        for j in range(dom_size):
            for r in range(rep_size):
                owner = (r * owners_here + (k + j) % owners_here) * rep_size + j // owners_here
                pairs.append((j * rep_size + r, owner))
        return pairs

    label_rows = labels.astype(jnp.float32).reshape(owners_here, per_owner)
    sent_at = (dom_at % owners_here - chunk_ids) % owners_here
    label_part = jnp.concatenate(
        [
            lax.ppermute(label_rows[sent_at[k]], ("dom", "rep"), [(b, a) for a, b in score_pairs(k)])
            for k in range(owners_here)
        ]
    )

    pre = lax.dot_general(
        inputs, w_first, (((0,), (0,)), ((), ())), preferred_element_type=jnp.float32
    )
    gate = jax.nn.sigmoid(pre)
    scores = jnp.dot(pre * gate, w_score, precision=lax.Precision.HIGHEST)
    error_term = jax.nn.sigmoid(scores) - label_part
    derivative = gate * (1.0 + pre * (1.0 - gate))
    back = (error_term[:, None] * w_score[None, :] * derivative).astype(jnp.bfloat16)
    local_grad = jnp.dot(inputs, back, preferred_element_type=jnp.float32)
    gradient = reduce_rows(local_grad, dom_size, rep_size)

    score_rows = scores.reshape(owners_here, per_owner)
    returned = jnp.stack(
        [lax.ppermute(score_rows[k], ("dom", "rep"), score_pairs(k)) for k in range(owners_here)]
    )
    own_scores = jnp.take(returned, sent_at, axis=0).reshape(per_dev)
    return (hop_out, own_scores, gradient)


def solution(mesh):
    placed = (
        P("rep", "dom"),
        P("dom", "rep", None, None),
        P("dom", None),
        P("dom", None),
        P("dom", None),
        P(("dom", "rep")),
        P(),
        P(),
    )
    return jax.shard_map(
        on_device,
        mesh=mesh,
        in_specs=placed,
        out_specs=(P("rep", "dom"), P(("dom", "rep")), P("rep", None)),
        check_vma=False,
    )
```

```python
import jax
import jax.numpy as jnp
from jax import lax
from jax.sharding import PartitionSpec as P


def hop_terms(source_rows, tile_piece, spread):
    product_terms = jnp.einsum(
        "jfc,jrc->jfr", source_rows, tile_piece.astype(jnp.float32), precision=lax.Precision.HIGHEST
    )
    return jnp.einsum("jb,jfr->fbr", spread, product_terms, precision=lax.Precision.HIGHEST)


def gather_all(values, axes, count):
    copies = jnp.broadcast_to(values[None], (count,) + values.shape)
    return lax.all_to_all(copies, axes, 0, 0, tiled=True).reshape((count * values.shape[0],) + values.shape[1:])


def halve_in_order(values, steps, bit_names, sizes):
    names = list(bit_names)
    values = values.reshape((2,) * len(names) + (values.shape[0] >> len(names),) + values.shape[1:])
    for name in steps:
        axis, bit_at = name
        position = names.index(name)
        bit = (lax.axis_index(axis) >> bit_at) & 1
        keep = lax.dynamic_index_in_dim(values, bit, position, keepdims=False)
        give = lax.dynamic_index_in_dim(values, 1 - bit, position, keepdims=False)
        pairs = [(i, i ^ (1 << bit_at)) for i in range(sizes[axis])]
        values = keep + lax.ppermute(give, axis, pairs)
        names.pop(position)
    return values


def double(values, axis, size):
    index = lax.axis_index(axis)
    values = values[None]
    step = size.bit_length() - 2
    while step >= 0:
        bit = (index >> step) & 1
        got = lax.ppermute(values, axis, [(i, i ^ (1 << step)) for i in range(size)])
        low, high = jnp.where(bit == 0, values, got), jnp.where(bit == 0, got, values)
        values = jnp.stack([low, high], axis=1).reshape((values.shape[0] * 2,) + values.shape[1:])
        step -= 1
    return values.reshape((-1,) + values.shape[2:])


def reduce_rows(local_grad, dom_size, rep_size):
    rows, cols = local_grad.shape
    piece = rows // (rep_size * dom_size)
    if rep_size & (rep_size - 1) == 0 and dom_size & (dom_size - 1) == 0 and cols % 2 == 0:
        rep_bits = [("rep", b) for b in range(rep_size.bit_length() - 1)]
        dom_bits = [("dom", b) for b in range(dom_size.bit_length() - 1)]
        bit_names = rep_bits[::-1] + dom_bits[::-1]
        sizes = {"rep": rep_size, "dom": dom_size}
        first = halve_in_order(local_grad[:, : cols // 2], rep_bits + dom_bits, bit_names, sizes)
        second = halve_in_order(local_grad[:, cols // 2 :], rep_bits[:1] + dom_bits + rep_bits[1:], bit_names, sizes)
        return jnp.concatenate([double(first, "dom", dom_size), double(second, "dom", dom_size)], axis=-1)
    else:
        parts = local_grad.reshape(rep_size, dom_size, piece, cols)
        parts = lax.all_to_all(parts, "rep", 0, 0, tiled=True).sum(0)
        parts = lax.all_to_all(parts, "dom", 0, 0, tiled=True).sum(0)
    return gather_all(parts, "dom", dom_size)


def on_device(features_t, tiles, send_block, tile_row, order, labels, w_first, w_score):
    feat_cols, row_count = features_t.shape
    tile_size = tiles.shape[-1]
    block_count = row_count // tile_size
    dom_size = lax.axis_size("dom")
    rep_size = lax.axis_size("rep")
    dom_at = lax.axis_index("dom")
    rep_at = lax.axis_index("rep")
    node_blocks = features_t.reshape(feat_cols, block_count, tile_size)
    block_ids = jnp.arange(block_count, dtype=jnp.int32)
    sent = (send_block[0][:, None] == block_ids[None, :]).astype(jnp.float32)
    outgoing = jnp.einsum("fbc,jb->jfc", node_blocks, sent, precision=lax.Precision.HIGHEST)
    placed = (tile_row[0][:, None] == block_ids[None, :]).astype(jnp.float32)
    local_tiles = tiles[0]
    arrived = lax.all_to_all(outgoing, "dom", split_axis=0, concat_axis=0, tiled=True)
    hopped = hop_terms(arrived, lax.all_gather(local_tiles, "rep", axis=0, tiled=True), placed)
    hop_out = hopped.reshape(feat_cols, row_count)

    per_dev = labels.shape[0]
    per_owner = row_count // dom_size
    owners_here = per_dev // per_owner
    chunk_ids = jnp.arange(owners_here, dtype=jnp.int32)
    rotated = (chunk_ids + dom_at) % owners_here
    node_ids = order[0].reshape(rep_size, owners_here, per_owner)
    node_ids = jnp.take(node_ids, rotated, axis=1).reshape(row_count)
    rows_here = jnp.concatenate([features_t.astype(jnp.bfloat16), hop_out.astype(jnp.bfloat16)], axis=0)
    select = (jnp.arange(row_count, dtype=jnp.int32)[:, None] == node_ids[None, :]).astype(jnp.bfloat16)
    picked = jnp.einsum(
        "fn,nrq->rfq", rows_here, select.reshape(row_count, rep_size, per_dev), preferred_element_type=jnp.float32
    ).astype(jnp.bfloat16)
    got = lax.all_to_all(picked, "rep", split_axis=0, concat_axis=0, tiled=True)
    inputs = got.reshape(rep_size, 2, feat_cols, per_dev).transpose(1, 0, 2, 3).reshape(-1, per_dev)

    def score_pairs(k):
        pairs = []
        for j in range(dom_size):
            for r in range(rep_size):
                owner = (r * owners_here + (k + j) % owners_here) * rep_size + j // owners_here
                pairs.append((j * rep_size + r, owner))
        return pairs

    label_rows = labels.astype(jnp.float32).reshape(owners_here, per_owner)
    sent_at = (dom_at % owners_here - chunk_ids) % owners_here
    label_part = jnp.concatenate(
        [
            lax.ppermute(label_rows[sent_at[k]], ("dom", "rep"), [(b, a) for a, b in score_pairs(k)])
            for k in range(owners_here)
        ]
    )

    pre = lax.dot_general(
        inputs, w_first, (((0,), (0,)), ((), ())), preferred_element_type=jnp.float32
    )
    gate = jax.nn.sigmoid(pre)
    scores = jnp.dot(pre * gate, w_score, precision=lax.Precision.HIGHEST)
    error_term = jax.nn.sigmoid(scores) - label_part
    derivative = gate * (1.0 + pre * (1.0 - gate))
    back = (error_term[:, None] * w_score[None, :] * derivative).astype(jnp.bfloat16)
    local_grad = jnp.dot(inputs, back, preferred_element_type=jnp.float32)
    gradient = reduce_rows(local_grad, dom_size, rep_size)

    score_rows = scores.reshape(owners_here, per_owner)
    returned = jnp.stack(
        [lax.ppermute(score_rows[k], ("dom", "rep"), score_pairs(k)) for k in range(owners_here)]
    )
    own_scores = jnp.take(returned, sent_at, axis=0).reshape(per_dev)
    return (hop_out, own_scores, gradient)


def solution(mesh):
    placed = (
        P("rep", "dom"),
        P("dom", "rep", None, None),
        P("dom", None),
        P("dom", None),
        P("dom", None),
        P(("dom", "rep")),
        P(),
        P(),
    )
    return jax.shard_map(
        on_device,
        mesh=mesh,
        in_specs=placed,
        out_specs=(P("rep", "dom"), P(("dom", "rep")), P("rep", None)),
        check_vma=False,
    )
```

```python
import jax
import jax.numpy as jnp
from jax import lax
from jax.sharding import PartitionSpec as P


def hop_terms(source_rows, tile_piece, spread):
    product_terms = jnp.einsum(
        "jfc,jrc->jfr", source_rows, tile_piece.astype(jnp.float32), precision=lax.Precision.HIGHEST
    )
    return jnp.einsum("jb,jfr->fbr", spread, product_terms, precision=lax.Precision.HIGHEST)


def gather_all(values, axes, count):
    copies = jnp.broadcast_to(values[None], (count,) + values.shape)
    return lax.all_to_all(copies, axes, 0, 0, tiled=True).reshape((count * values.shape[0],) + values.shape[1:])


def halve_in_order(values, steps, bit_names, sizes):
    names = list(bit_names)
    values = values.reshape((2,) * len(names) + (values.shape[0] >> len(names),) + values.shape[1:])
    for name in steps:
        axis, bit_at = name
        position = names.index(name)
        bit = (lax.axis_index(axis) >> bit_at) & 1
        keep = lax.dynamic_index_in_dim(values, bit, position, keepdims=False)
        give = lax.dynamic_index_in_dim(values, 1 - bit, position, keepdims=False)
        pairs = [(i, i ^ (1 << bit_at)) for i in range(sizes[axis])]
        values = keep + lax.ppermute(give, axis, pairs)
        names.pop(position)
    return values


def reduce_rows(local_grad, dom_size, rep_size):
    rows, cols = local_grad.shape
    piece = rows // (rep_size * dom_size)
    if rep_size & (rep_size - 1) == 0 and dom_size & (dom_size - 1) == 0 and cols % 2 == 0:
        rep_bits = [("rep", b) for b in range(rep_size.bit_length() - 1)]
        dom_bits = [("dom", b) for b in range(dom_size.bit_length() - 1)]
        bit_names = rep_bits[::-1] + dom_bits[::-1]
        sizes = {"rep": rep_size, "dom": dom_size}
        first = halve_in_order(local_grad[:, : cols // 2], rep_bits + dom_bits, bit_names, sizes)
        second = halve_in_order(local_grad[:, cols // 2 :], rep_bits[:1] + dom_bits + rep_bits[1:], bit_names, sizes)
        parts = jnp.concatenate([first, second], axis=-1)
    else:
        parts = local_grad.reshape(rep_size, dom_size, piece, cols)
        parts = lax.all_to_all(parts, "rep", 0, 0, tiled=True).sum(0)
        parts = lax.all_to_all(parts, "dom", 0, 0, tiled=True).sum(0)
    return gather_all(parts, "dom", dom_size)


def on_device(features_t, tiles, send_block, tile_row, order, labels, w_first, w_score):
    feat_cols, row_count = features_t.shape
    tile_size = tiles.shape[-1]
    block_count = row_count // tile_size
    dom_size = lax.axis_size("dom")
    rep_size = lax.axis_size("rep")
    dom_at = lax.axis_index("dom")
    rep_at = lax.axis_index("rep")
    node_blocks = features_t.reshape(feat_cols, block_count, tile_size)
    block_ids = jnp.arange(block_count, dtype=jnp.int32)
    outgoing = jnp.take(node_blocks, send_block[0], axis=1).transpose(1, 0, 2)
    placed = (tile_row[0][:, None] == block_ids[None, :]).astype(jnp.float32)
    local_tiles = tiles[0]
    arrived = lax.all_to_all(outgoing, "dom", split_axis=0, concat_axis=0, tiled=True)
    hopped = hop_terms(arrived, lax.all_gather(local_tiles, "rep", axis=0, tiled=True), placed)
    hop_out = hopped.reshape(feat_cols, row_count)

    per_dev = labels.shape[0]
    per_owner = row_count // dom_size
    owners_here = per_dev // per_owner
    chunk_ids = jnp.arange(owners_here, dtype=jnp.int32)
    rotated = (chunk_ids + dom_at) % owners_here
    node_ids = order[0].reshape(rep_size, owners_here, per_owner)
    node_ids = jnp.take(node_ids, rotated, axis=1).reshape(row_count)
    rows_here = jnp.concatenate([features_t.astype(jnp.bfloat16), hop_out.astype(jnp.bfloat16)], axis=0)
    select = (jnp.arange(row_count, dtype=jnp.int32)[:, None] == node_ids[None, :]).astype(jnp.bfloat16)
    picked = jnp.einsum(
        "fn,nrq->rfq", rows_here, select.reshape(row_count, rep_size, per_dev), preferred_element_type=jnp.float32
    ).astype(jnp.bfloat16)
    got = lax.all_to_all(picked, "rep", split_axis=0, concat_axis=0, tiled=True)
    inputs = got.reshape(rep_size, 2, feat_cols, per_dev).transpose(1, 0, 2, 3).reshape(-1, per_dev)

    def score_pairs(k):
        pairs = []
        for j in range(dom_size):
            for r in range(rep_size):
                owner = (r * owners_here + (k + j) % owners_here) * rep_size + j // owners_here
                pairs.append((j * rep_size + r, owner))
        return pairs

    label_rows = labels.astype(jnp.float32).reshape(owners_here, per_owner)
    sent_at = (dom_at % owners_here - chunk_ids) % owners_here
    label_part = jnp.concatenate(
        [
            lax.ppermute(label_rows[sent_at[k]], ("dom", "rep"), [(b, a) for a, b in score_pairs(k)])
            for k in range(owners_here)
        ]
    )

    pre = lax.dot_general(
        inputs, w_first, (((0,), (0,)), ((), ())), preferred_element_type=jnp.float32
    )
    gate = jax.nn.sigmoid(pre)
    scores = jnp.dot(pre * gate, w_score, precision=lax.Precision.HIGHEST)
    error_term = jax.nn.sigmoid(scores) - label_part
    derivative = gate * (1.0 + pre * (1.0 - gate))
    back = (error_term[:, None] * w_score[None, :] * derivative).astype(jnp.bfloat16)
    local_grad = jnp.dot(inputs, back, preferred_element_type=jnp.float32)
    gradient = reduce_rows(local_grad, dom_size, rep_size)

    score_rows = scores.reshape(owners_here, per_owner)
    returned = jnp.stack(
        [lax.ppermute(score_rows[k], ("dom", "rep"), score_pairs(k)) for k in range(owners_here)]
    )
    own_scores = jnp.take(returned, sent_at, axis=0).reshape(per_dev)
    return (hop_out, own_scores, gradient)


def solution(mesh):
    placed = (
        P("rep", "dom"),
        P("dom", "rep", None, None),
        P("dom", None),
        P("dom", None),
        P("dom", None),
        P(("dom", "rep")),
        P(),
        P(),
    )
    return jax.shard_map(
        on_device,
        mesh=mesh,
        in_specs=placed,
        out_specs=(P("rep", "dom"), P(("dom", "rep")), P("rep", None)),
        check_vma=False,
    )
```

```python
import jax
import jax.numpy as jnp
from jax import lax
from jax.sharding import PartitionSpec as P


def hop_terms(source_rows, tile_piece, spread):
    product_terms = jnp.einsum(
        "jfc,jrc->jfr", source_rows, tile_piece.astype(jnp.float32), precision=lax.Precision.HIGHEST
    )
    return jnp.einsum("jb,jfr->fbr", spread, product_terms, precision=lax.Precision.HIGHEST)


def gather_all(values, axes, count):
    copies = jnp.broadcast_to(values[None], (count,) + values.shape)
    return lax.all_to_all(copies, axes, 0, 0, tiled=True).reshape((count * values.shape[0],) + values.shape[1:])


def halve_in_order(values, steps, bit_names, sizes):
    names = list(bit_names)
    values = values.reshape((2,) * len(names) + (values.shape[0] >> len(names),) + values.shape[1:])
    for name in steps:
        axis, bit_at = name
        position = names.index(name)
        bit = (lax.axis_index(axis) >> bit_at) & 1
        keep = lax.dynamic_index_in_dim(values, bit, position, keepdims=False)
        give = lax.dynamic_index_in_dim(values, 1 - bit, position, keepdims=False)
        pairs = [(i, i ^ (1 << bit_at)) for i in range(sizes[axis])]
        values = keep + lax.ppermute(give, axis, pairs)
        names.pop(position)
    return values


def reduce_rows(local_grad, dom_size, rep_size):
    rows, cols = local_grad.shape
    piece = rows // (rep_size * dom_size)
    if rep_size & (rep_size - 1) == 0 and dom_size & (dom_size - 1) == 0 and cols % 2 == 0:
        rep_bits = [("rep", b) for b in range(rep_size.bit_length() - 1)]
        dom_bits = [("dom", b) for b in range(dom_size.bit_length() - 1)]
        bit_names = rep_bits[::-1] + dom_bits[::-1]
        sizes = {"rep": rep_size, "dom": dom_size}
        first = halve_in_order(local_grad[:, : cols // 2], rep_bits + dom_bits, bit_names, sizes)
        second = halve_in_order(local_grad[:, cols // 2 :], rep_bits[:1] + dom_bits + rep_bits[1:], bit_names, sizes)
        parts = jnp.concatenate([first, second], axis=-1)
    else:
        parts = local_grad.reshape(rep_size, dom_size, piece, cols)
        parts = lax.all_to_all(parts, "rep", 0, 0, tiled=True).sum(0)
        parts = lax.all_to_all(parts, "dom", 0, 0, tiled=True).sum(0)
    return gather_all(parts, "dom", dom_size)


def on_device(features_t, tiles, send_block, tile_row, order, labels, w_first, w_score):
    feat_cols, row_count = features_t.shape
    tile_size = tiles.shape[-1]
    block_count = row_count // tile_size
    dom_size = lax.axis_size("dom")
    rep_size = lax.axis_size("rep")
    dom_at = lax.axis_index("dom")
    rep_at = lax.axis_index("rep")
    node_blocks = features_t.reshape(feat_cols, block_count, tile_size)
    block_ids = jnp.arange(block_count, dtype=jnp.int32)
    sent = (send_block[0][:, None] == block_ids[None, :]).astype(jnp.float32)
    outgoing = jnp.einsum("fbc,jb->jfc", node_blocks, sent, precision=lax.Precision.HIGHEST)
    placed = (tile_row[0][:, None] == block_ids[None, :]).astype(jnp.float32)
    local_tiles = tiles[0]
    arrived = lax.all_to_all(outgoing, "dom", split_axis=0, concat_axis=0, tiled=True)
    per_dev = labels.shape[0]
    per_owner = row_count // dom_size
    owners_here = per_dev // per_owner
    chunk_ids = jnp.arange(owners_here, dtype=jnp.int32)
    def score_pairs(k):
        pairs = []
        for j in range(dom_size):
            for r in range(rep_size):
                owner = (r * owners_here + (k + j) % owners_here) * rep_size + j // owners_here
                pairs.append((j * rep_size + r, owner))
        return pairs

    label_rows = labels.astype(jnp.float32).reshape(owners_here, per_owner)
    sent_at = (dom_at % owners_here - chunk_ids) % owners_here
    label_part = jnp.concatenate(
        [
            lax.ppermute(label_rows[sent_at[k]], ("dom", "rep"), [(b, a) for a, b in score_pairs(k)])
            for k in range(owners_here)
        ]
    )

    label_part, arrived = lax.optimization_barrier((label_part, arrived))
    hopped = hop_terms(arrived, lax.all_gather(local_tiles, "rep", axis=0, tiled=True), placed)
    hop_out = hopped.reshape(feat_cols, row_count)

    rotated = (chunk_ids + dom_at) % owners_here
    node_ids = order[0].reshape(rep_size, owners_here, per_owner)
    node_ids = jnp.take(node_ids, rotated, axis=1).reshape(row_count)
    rows_here = jnp.concatenate([features_t.astype(jnp.bfloat16), hop_out.astype(jnp.bfloat16)], axis=0)
    select = (jnp.arange(row_count, dtype=jnp.int32)[:, None] == node_ids[None, :]).astype(jnp.bfloat16)
    picked = jnp.einsum(
        "fn,nrq->rfq", rows_here, select.reshape(row_count, rep_size, per_dev), preferred_element_type=jnp.float32
    ).astype(jnp.bfloat16)
    got = lax.all_to_all(picked, "rep", split_axis=0, concat_axis=0, tiled=True)
    inputs = got.reshape(rep_size, 2, feat_cols, per_dev).transpose(1, 0, 2, 3).reshape(-1, per_dev)

    pre = lax.dot_general(
        inputs, w_first, (((0,), (0,)), ((), ())), preferred_element_type=jnp.float32
    )
    gate = jax.nn.sigmoid(pre)
    scores = jnp.dot(pre * gate, w_score, precision=lax.Precision.HIGHEST)
    error_term = jax.nn.sigmoid(scores) - label_part
    derivative = gate * (1.0 + pre * (1.0 - gate))
    back = (error_term[:, None] * w_score[None, :] * derivative).astype(jnp.bfloat16)
    local_grad = jnp.dot(inputs, back, preferred_element_type=jnp.float32)
    gradient = reduce_rows(local_grad, dom_size, rep_size)

    score_rows = scores.reshape(owners_here, per_owner)
    returned = jnp.stack(
        [lax.ppermute(score_rows[k], ("dom", "rep"), score_pairs(k)) for k in range(owners_here)]
    )
    own_scores = jnp.take(returned, sent_at, axis=0).reshape(per_dev)
    return (hop_out, own_scores, gradient)


def solution(mesh):
    placed = (
        P("rep", "dom"),
        P("dom", "rep", None, None),
        P("dom", None),
        P("dom", None),
        P("dom", None),
        P(("dom", "rep")),
        P(),
        P(),
    )
    return jax.shard_map(
        on_device,
        mesh=mesh,
        in_specs=placed,
        out_specs=(P("rep", "dom"), P(("dom", "rep")), P("rep", None)),
        check_vma=False,
    )
```

```python
import jax
import jax.numpy as jnp
from jax import lax
from jax.sharding import PartitionSpec as P


def hop_terms(source_rows, tile_piece, spread):
    product_terms = jnp.einsum(
        "jfc,jrc->jfr", source_rows, tile_piece.astype(jnp.float32), precision=lax.Precision.HIGHEST
    )
    return jnp.einsum("jb,jfr->fbr", spread, product_terms, precision=lax.Precision.HIGHEST)


def gather_all(values, axes, count):
    copies = jnp.broadcast_to(values[None], (count,) + values.shape)
    return lax.all_to_all(copies, axes, 0, 0, tiled=True).reshape((count * values.shape[0],) + values.shape[1:])


def halve_in_order(values, steps, bit_names, sizes):
    names = list(bit_names)
    values = values.reshape((2,) * len(names) + (values.shape[0] >> len(names),) + values.shape[1:])
    for name in steps:
        axis, bit_at = name
        position = names.index(name)
        bit = (lax.axis_index(axis) >> bit_at) & 1
        keep = lax.dynamic_index_in_dim(values, bit, position, keepdims=False)
        give = lax.dynamic_index_in_dim(values, 1 - bit, position, keepdims=False)
        pairs = [(i, i ^ (1 << bit_at)) for i in range(sizes[axis])]
        values = keep + lax.ppermute(give, axis, pairs)
        names.pop(position)
    return values


def reduce_rows(local_grad, dom_size, rep_size):
    rows, cols = local_grad.shape
    piece = rows // (rep_size * dom_size)
    if rep_size & (rep_size - 1) == 0 and dom_size & (dom_size - 1) == 0 and cols % 2 == 0:
        rep_bits = [("rep", b) for b in range(rep_size.bit_length() - 1)]
        dom_bits = [("dom", b) for b in range(dom_size.bit_length() - 1)]
        bit_names = rep_bits[::-1] + dom_bits[::-1]
        sizes = {"rep": rep_size, "dom": dom_size}
        summed = halve_in_order(local_grad, rep_bits[:1], bit_names, sizes)
        summed = summed.reshape(rows // 2, cols)
        bit_names = rep_bits[:0:-1] + dom_bits[::-1]
        first = halve_in_order(summed[:, : cols // 2], rep_bits[1:] + dom_bits, bit_names, sizes)
        second = halve_in_order(summed[:, cols // 2 :], dom_bits + rep_bits[1:], bit_names, sizes)
        parts = jnp.concatenate([first, second], axis=-1)
    else:
        parts = local_grad.reshape(rep_size, dom_size, piece, cols)
        parts = lax.all_to_all(parts, "rep", 0, 0, tiled=True).sum(0)
        parts = lax.all_to_all(parts, "dom", 0, 0, tiled=True).sum(0)
    return gather_all(parts, "dom", dom_size)


def on_device(features_t, tiles, send_block, tile_row, order, labels, w_first, w_score):
    feat_cols, row_count = features_t.shape
    tile_size = tiles.shape[-1]
    block_count = row_count // tile_size
    dom_size = lax.axis_size("dom")
    rep_size = lax.axis_size("rep")
    dom_at = lax.axis_index("dom")
    rep_at = lax.axis_index("rep")
    node_blocks = features_t.reshape(feat_cols, block_count, tile_size)
    block_ids = jnp.arange(block_count, dtype=jnp.int32)
    sent = (send_block[0][:, None] == block_ids[None, :]).astype(jnp.float32)
    outgoing = jnp.einsum("fbc,jb->jfc", node_blocks, sent, precision=lax.Precision.HIGHEST)
    placed = (tile_row[0][:, None] == block_ids[None, :]).astype(jnp.float32)
    local_tiles = tiles[0]
    arrived = lax.all_to_all(outgoing, "dom", split_axis=0, concat_axis=0, tiled=True)
    hopped = hop_terms(arrived, lax.all_gather(local_tiles, "rep", axis=0, tiled=True), placed)
    hop_out = hopped.reshape(feat_cols, row_count)

    per_dev = labels.shape[0]
    per_owner = row_count // dom_size
    owners_here = per_dev // per_owner
    chunk_ids = jnp.arange(owners_here, dtype=jnp.int32)
    rotated = (chunk_ids + dom_at) % owners_here
    node_ids = order[0].reshape(rep_size, owners_here, per_owner)
    node_ids = jnp.take(node_ids, rotated, axis=1).reshape(row_count)
    rows_here = jnp.concatenate([features_t.astype(jnp.bfloat16), hop_out.astype(jnp.bfloat16)], axis=0)
    select = (jnp.arange(row_count, dtype=jnp.int32)[:, None] == node_ids[None, :]).astype(jnp.bfloat16)
    picked = jnp.einsum(
        "fn,nrq->rfq", rows_here, select.reshape(row_count, rep_size, per_dev), preferred_element_type=jnp.float32
    ).astype(jnp.bfloat16)
    got = lax.all_to_all(picked, "rep", split_axis=0, concat_axis=0, tiled=True)
    inputs = got.reshape(rep_size, 2, feat_cols, per_dev).transpose(1, 0, 2, 3).reshape(-1, per_dev)

    def score_pairs(k):
        pairs = []
        for j in range(dom_size):
            for r in range(rep_size):
                owner = (r * owners_here + (k + j) % owners_here) * rep_size + j // owners_here
                pairs.append((j * rep_size + r, owner))
        return pairs

    label_rows = labels.astype(jnp.float32).reshape(owners_here, per_owner)
    sent_at = (dom_at % owners_here - chunk_ids) % owners_here
    label_part = jnp.concatenate(
        [
            lax.ppermute(label_rows[sent_at[k]], ("dom", "rep"), [(b, a) for a, b in score_pairs(k)])
            for k in range(owners_here)
        ]
    )

    pre = lax.dot_general(
        inputs, w_first, (((0,), (0,)), ((), ())), preferred_element_type=jnp.float32
    )
    gate = jax.nn.sigmoid(pre)
    scores = jnp.dot(pre * gate, w_score, precision=lax.Precision.HIGHEST)
    error_term = jax.nn.sigmoid(scores) - label_part
    derivative = gate * (1.0 + pre * (1.0 - gate))
    back = (error_term[:, None] * w_score[None, :] * derivative).astype(jnp.bfloat16)
    local_grad = jnp.dot(inputs, back, preferred_element_type=jnp.float32)
    gradient = reduce_rows(local_grad, dom_size, rep_size)

    score_rows = scores.reshape(owners_here, per_owner)
    returned = jnp.stack(
        [lax.ppermute(score_rows[k], ("dom", "rep"), score_pairs(k)) for k in range(owners_here)]
    )
    own_scores = jnp.take(returned, sent_at, axis=0).reshape(per_dev)
    return (hop_out, own_scores, gradient)


def solution(mesh):
    placed = (
        P("rep", "dom"),
        P("dom", "rep", None, None),
        P("dom", None),
        P("dom", None),
        P("dom", None),
        P(("dom", "rep")),
        P(),
        P(),
    )
    return jax.shard_map(
        on_device,
        mesh=mesh,
        in_specs=placed,
        out_specs=(P("rep", "dom"), P(("dom", "rep")), P("rep", None)),
        check_vma=False,
    )
```

```python
import jax
import jax.numpy as jnp
from jax import lax
from jax.sharding import PartitionSpec as P


def hop_terms(source_rows, tile_piece, spread):
    product_terms = jnp.einsum(
        "jfc,jrc->jfr", source_rows, tile_piece.astype(jnp.float32), precision=lax.Precision.HIGHEST
    )
    return jnp.einsum("jb,jfr->fbr", spread, product_terms, precision=lax.Precision.HIGHEST)


def gather_all(values, axes, count):
    copies = jnp.broadcast_to(values[None], (count,) + values.shape)
    return lax.all_to_all(copies, axes, 0, 0, tiled=True).reshape((count * values.shape[0],) + values.shape[1:])


def halve_in_order(values, steps, bit_names, sizes):
    names = list(bit_names)
    values = values.reshape((2,) * len(names) + (values.shape[0] >> len(names),) + values.shape[1:])
    for name in steps:
        axis, bit_at = name
        position = names.index(name)
        bit = (lax.axis_index(axis) >> bit_at) & 1
        keep = lax.dynamic_index_in_dim(values, bit, position, keepdims=False)
        give = lax.dynamic_index_in_dim(values, 1 - bit, position, keepdims=False)
        pairs = [(i, i ^ (1 << bit_at)) for i in range(sizes[axis])]
        values = keep + lax.ppermute(give, axis, pairs)
        names.pop(position)
    return values


def reduce_rows(local_grad, dom_size, rep_size):
    rows, cols = local_grad.shape
    piece = rows // (rep_size * dom_size)
    if rep_size & (rep_size - 1) == 0 and dom_size & (dom_size - 1) == 0 and cols % 2 == 0:
        rep_bits = [("rep", b) for b in range(rep_size.bit_length() - 1)]
        dom_bits = [("dom", b) for b in range(dom_size.bit_length() - 1)]
        bit_names = rep_bits[::-1] + dom_bits[::-1]
        sizes = {"rep": rep_size, "dom": dom_size}
        first = halve_in_order(local_grad[:, : cols // 2], rep_bits + dom_bits, bit_names, sizes)
        second = halve_in_order(local_grad[:, cols // 2 :], rep_bits[:1] + dom_bits + rep_bits[1:], bit_names, sizes)
        parts = jnp.concatenate([first, second], axis=-1)
    else:
        parts = local_grad.reshape(rep_size, dom_size, piece, cols)
        parts = lax.all_to_all(parts, "rep", 0, 0, tiled=True).sum(0)
        parts = lax.all_to_all(parts, "dom", 0, 0, tiled=True).sum(0)
    return gather_all(parts, "dom", dom_size)


def on_device(features_t, tiles, send_block, tile_row, order, labels, w_first, w_score):
    feat_cols, row_count = features_t.shape
    tile_size = tiles.shape[-1]
    block_count = row_count // tile_size
    dom_size = lax.axis_size("dom")
    rep_size = lax.axis_size("rep")
    dom_at = lax.axis_index("dom")
    rep_at = lax.axis_index("rep")
    node_blocks = features_t.reshape(feat_cols, block_count, tile_size)
    block_ids = jnp.arange(block_count, dtype=jnp.int32)
    sent = (send_block[0][:, None] == block_ids[None, :]).astype(jnp.float32)
    outgoing = jnp.einsum("fbc,jb->jfc", node_blocks, sent, precision=lax.Precision.HIGHEST)
    placed = (tile_row[0][:, None] == block_ids[None, :]).astype(jnp.float32)
    local_tiles = tiles[0]
    arrived = lax.all_to_all(outgoing, "dom", split_axis=0, concat_axis=0, tiled=True)
    hopped = hop_terms(arrived, lax.all_gather(local_tiles, "rep", axis=0, tiled=True), placed)
    hop_out = hopped.reshape(feat_cols, row_count)

    per_dev = labels.shape[0]
    per_owner = row_count // dom_size
    owners_here = per_dev // per_owner
    chunk_ids = jnp.arange(owners_here, dtype=jnp.int32)
    rotated = (chunk_ids + dom_at) % owners_here
    node_ids = order[0].reshape(rep_size, owners_here, per_owner)
    node_ids = jnp.take(node_ids, rotated, axis=1).reshape(row_count)
    rows_here = jnp.concatenate([features_t.astype(jnp.bfloat16), hop_out.astype(jnp.bfloat16)], axis=0)
    select = (jnp.arange(row_count, dtype=jnp.int32)[:, None] == node_ids[None, :]).astype(jnp.bfloat16)
    picked = jnp.einsum(
        "fn,nrq->rfq", rows_here, select.reshape(row_count, rep_size, per_dev), preferred_element_type=jnp.float32
    ).astype(jnp.bfloat16)
    got = lax.all_to_all(picked, "rep", split_axis=0, concat_axis=0, tiled=True)
    inputs = got.reshape(rep_size, 2, feat_cols, per_dev).transpose(1, 0, 2, 3).reshape(-1, per_dev)

    def score_pairs(k):
        pairs = []
        for j in range(dom_size):
            for r in range(rep_size):
                owner = (r * owners_here + (k + j) % owners_here) * rep_size + j // owners_here
                pairs.append((j * rep_size + r, owner))
        return pairs

    sent_at = (dom_at % owners_here - chunk_ids) % owners_here
    all_labels = gather_all(labels.astype(jnp.float32), ("dom", "rep"), dom_size * rep_size)
    all_labels = all_labels.reshape(dom_size, dom_size, per_owner)
    label_part = jnp.stack(
        [
            lax.dynamic_slice(all_labels, (rep_at * owners_here + (k + dom_at) % owners_here, dom_at, 0), (1, 1, per_owner))
            for k in range(owners_here)
        ]
    ).reshape(per_dev)

    pre = lax.dot_general(
        inputs, w_first, (((0,), (0,)), ((), ())), preferred_element_type=jnp.float32
    )
    gate = jax.nn.sigmoid(pre)
    scores = jnp.dot(pre * gate, w_score, precision=lax.Precision.HIGHEST)
    error_term = jax.nn.sigmoid(scores) - label_part
    derivative = gate * (1.0 + pre * (1.0 - gate))
    back = (error_term[:, None] * w_score[None, :] * derivative).astype(jnp.bfloat16)
    local_grad = jnp.dot(inputs, back, preferred_element_type=jnp.float32)
    gradient = reduce_rows(local_grad, dom_size, rep_size)

    score_rows = scores.reshape(owners_here, per_owner)
    returned = jnp.stack(
        [lax.ppermute(score_rows[k], ("dom", "rep"), score_pairs(k)) for k in range(owners_here)]
    )
    own_scores = jnp.take(returned, sent_at, axis=0).reshape(per_dev)
    return (hop_out, own_scores, gradient)


def solution(mesh):
    placed = (
        P("rep", "dom"),
        P("dom", "rep", None, None),
        P("dom", None),
        P("dom", None),
        P("dom", None),
        P(("dom", "rep")),
        P(),
        P(),
    )
    return jax.shard_map(
        on_device,
        mesh=mesh,
        in_specs=placed,
        out_specs=(P("rep", "dom"), P(("dom", "rep")), P("rep", None)),
        check_vma=False,
    )
```

```python
import jax
import jax.numpy as jnp
from jax import lax
from jax.sharding import PartitionSpec as P


def hop_terms(source_rows, tile_piece, spread):
    product_terms = jnp.einsum(
        "jfc,jrc->jfr", source_rows, tile_piece.astype(jnp.float32), precision=lax.Precision.HIGHEST
    )
    return jnp.einsum("jb,jfr->fbr", spread, product_terms, precision=lax.Precision.HIGHEST)


def gather_all(values, axes, count):
    copies = jnp.broadcast_to(values[None], (count,) + values.shape)
    return lax.all_to_all(copies, axes, 0, 0, tiled=True).reshape((count * values.shape[0],) + values.shape[1:])


def halve_in_order(values, steps, bit_names, sizes):
    names = list(bit_names)
    values = values.reshape((2,) * len(names) + (values.shape[0] >> len(names),) + values.shape[1:])
    for name in steps:
        axis, bit_at = name
        position = names.index(name)
        bit = (lax.axis_index(axis) >> bit_at) & 1
        keep = lax.dynamic_index_in_dim(values, bit, position, keepdims=False)
        give = lax.dynamic_index_in_dim(values, 1 - bit, position, keepdims=False)
        pairs = [(i, i ^ (1 << bit_at)) for i in range(sizes[axis])]
        values = keep + lax.ppermute(give, axis, pairs)
        names.pop(position)
    return values


def reduce_rows(local_grad, dom_size, rep_size):
    rows, cols = local_grad.shape
    piece = rows // (rep_size * dom_size)
    if rep_size & (rep_size - 1) == 0 and dom_size & (dom_size - 1) == 0 and cols % 2 == 0:
        rep_bits = [("rep", b) for b in range(rep_size.bit_length() - 1)]
        dom_bits = [("dom", b) for b in range(dom_size.bit_length() - 1)]
        bit_names = rep_bits[::-1] + dom_bits[::-1]
        sizes = {"rep": rep_size, "dom": dom_size}
        first = halve_in_order(local_grad[:, : cols // 2], rep_bits + dom_bits, bit_names, sizes)
        second = halve_in_order(local_grad[:, cols // 2 :], rep_bits[:1] + dom_bits + rep_bits[1:], bit_names, sizes)
        parts = jnp.concatenate([first, second], axis=-1)
    else:
        parts = local_grad.reshape(rep_size, dom_size, piece, cols)
        parts = lax.all_to_all(parts, "rep", 0, 0, tiled=True).sum(0)
        parts = lax.all_to_all(parts, "dom", 0, 0, tiled=True).sum(0)
    return lax.all_gather(parts, "dom", axis=0, tiled=True)


def on_device(features_t, tiles, send_block, tile_row, order, labels, w_first, w_score):
    feat_cols, row_count = features_t.shape
    tile_size = tiles.shape[-1]
    block_count = row_count // tile_size
    dom_size = lax.axis_size("dom")
    rep_size = lax.axis_size("rep")
    dom_at = lax.axis_index("dom")
    rep_at = lax.axis_index("rep")
    node_blocks = features_t.reshape(feat_cols, block_count, tile_size)
    block_ids = jnp.arange(block_count, dtype=jnp.int32)
    sent = (send_block[0][:, None] == block_ids[None, :]).astype(jnp.float32)
    outgoing = jnp.einsum("fbc,jb->jfc", node_blocks, sent, precision=lax.Precision.HIGHEST)
    placed = (tile_row[0][:, None] == block_ids[None, :]).astype(jnp.float32)
    local_tiles = tiles[0]
    arrived = lax.all_to_all(outgoing, "dom", split_axis=0, concat_axis=0, tiled=True)
    hopped = hop_terms(arrived, lax.all_gather(local_tiles, "rep", axis=0, tiled=True), placed)
    hop_out = hopped.reshape(feat_cols, row_count)

    per_dev = labels.shape[0]
    per_owner = row_count // dom_size
    owners_here = per_dev // per_owner
    chunk_ids = jnp.arange(owners_here, dtype=jnp.int32)
    rotated = (chunk_ids + dom_at) % owners_here
    node_ids = order[0].reshape(rep_size, owners_here, per_owner)
    node_ids = jnp.take(node_ids, rotated, axis=1).reshape(row_count)
    rows_here = jnp.concatenate([features_t.astype(jnp.bfloat16), hop_out.astype(jnp.bfloat16)], axis=0)
    select = (jnp.arange(row_count, dtype=jnp.int32)[:, None] == node_ids[None, :]).astype(jnp.bfloat16)
    picked = jnp.einsum(
        "fn,nrq->rfq", rows_here, select.reshape(row_count, rep_size, per_dev), preferred_element_type=jnp.float32
    ).astype(jnp.bfloat16)
    got = lax.all_to_all(picked, "rep", split_axis=0, concat_axis=0, tiled=True)
    inputs = got.reshape(rep_size, 2, feat_cols, per_dev).transpose(1, 0, 2, 3).reshape(-1, per_dev)

    def score_pairs(k):
        pairs = []
        for j in range(dom_size):
            for r in range(rep_size):
                owner = (r * owners_here + (k + j) % owners_here) * rep_size + j // owners_here
                pairs.append((j * rep_size + r, owner))
        return pairs

    label_rows = labels.astype(jnp.float32).reshape(owners_here, per_owner)
    sent_at = (dom_at % owners_here - chunk_ids) % owners_here
    label_part = jnp.concatenate(
        [
            lax.ppermute(label_rows[sent_at[k]], ("dom", "rep"), [(b, a) for a, b in score_pairs(k)])
            for k in range(owners_here)
        ]
    )

    pre = lax.dot_general(
        inputs, w_first, (((0,), (0,)), ((), ())), preferred_element_type=jnp.float32
    )
    gate = jax.nn.sigmoid(pre)
    scores = jnp.dot(pre * gate, w_score, precision=lax.Precision.HIGHEST)
    error_term = jax.nn.sigmoid(scores) - label_part
    derivative = gate * (1.0 + pre * (1.0 - gate))
    back = (error_term[:, None] * w_score[None, :] * derivative).astype(jnp.bfloat16)
    local_grad = jnp.dot(inputs, back, preferred_element_type=jnp.float32)
    gradient = reduce_rows(local_grad, dom_size, rep_size)

    score_rows = scores.reshape(owners_here, per_owner)
    returned = jnp.stack(
        [lax.ppermute(score_rows[k], ("dom", "rep"), score_pairs(k)) for k in range(owners_here)]
    )
    own_scores = jnp.take(returned, sent_at, axis=0).reshape(per_dev)
    return (hop_out, own_scores, gradient)


def solution(mesh):
    placed = (
        P("rep", "dom"),
        P("dom", "rep", None, None),
        P("dom", None),
        P("dom", None),
        P("dom", None),
        P(("dom", "rep")),
        P(),
        P(),
    )
    return jax.shard_map(
        on_device,
        mesh=mesh,
        in_specs=placed,
        out_specs=(P("rep", "dom"), P(("dom", "rep")), P("rep", None)),
        check_vma=False,
    )
```

```python
import jax
import jax.numpy as jnp
from jax import lax
from jax.sharding import PartitionSpec as P


def hop_terms(source_rows, tile_piece, spread):
    product_terms = jnp.einsum(
        "jfc,jrc->jfr", source_rows, tile_piece.astype(jnp.float32), precision=lax.Precision.HIGHEST
    )
    return jnp.einsum("jb,jfr->fbr", spread, product_terms, precision=lax.Precision.HIGHEST)


def gather_all(values, axes, count):
    copies = jnp.broadcast_to(values[None], (count,) + values.shape)
    return lax.all_to_all(copies, axes, 0, 0, tiled=True).reshape((count * values.shape[0],) + values.shape[1:])


def halve_in_order(values, steps, bit_names, sizes):
    names = list(bit_names)
    values = values.reshape((2,) * len(names) + (values.shape[0] >> len(names),) + values.shape[1:])
    for name in steps:
        axis, bit_at = name
        position = names.index(name)
        bit = (lax.axis_index(axis) >> bit_at) & 1
        keep = lax.dynamic_index_in_dim(values, bit, position, keepdims=False)
        give = lax.dynamic_index_in_dim(values, 1 - bit, position, keepdims=False)
        pairs = [(i, i ^ (1 << bit_at)) for i in range(sizes[axis])]
        values = keep + lax.ppermute(give, axis, pairs)
        names.pop(position)
    return values


def reduce_rows(local_grad, dom_size, rep_size):
    rows, cols = local_grad.shape
    piece = rows // (rep_size * dom_size)
    if rep_size & (rep_size - 1) == 0 and dom_size & (dom_size - 1) == 0 and cols % 2 == 0:
        rep_bits = [("rep", b) for b in range(rep_size.bit_length() - 1)]
        dom_bits = [("dom", b) for b in range(dom_size.bit_length() - 1)]
        bit_names = rep_bits[::-1] + dom_bits[::-1]
        sizes = {"rep": rep_size, "dom": dom_size}
        split = (cols * 5 // 8) // 128 * 128 or cols // 2
        first = halve_in_order(local_grad[:, :split], rep_bits + dom_bits, bit_names, sizes)
        second = halve_in_order(local_grad[:, split:], rep_bits[:1] + dom_bits + rep_bits[1:], bit_names, sizes)
        parts = jnp.concatenate([first, second], axis=-1)
    else:
        parts = local_grad.reshape(rep_size, dom_size, piece, cols)
        parts = lax.all_to_all(parts, "rep", 0, 0, tiled=True).sum(0)
        parts = lax.all_to_all(parts, "dom", 0, 0, tiled=True).sum(0)
    return gather_all(parts, "dom", dom_size)


def on_device(features_t, tiles, send_block, tile_row, order, labels, w_first, w_score):
    feat_cols, row_count = features_t.shape
    tile_size = tiles.shape[-1]
    block_count = row_count // tile_size
    dom_size = lax.axis_size("dom")
    rep_size = lax.axis_size("rep")
    dom_at = lax.axis_index("dom")
    rep_at = lax.axis_index("rep")
    node_blocks = features_t.reshape(feat_cols, block_count, tile_size)
    block_ids = jnp.arange(block_count, dtype=jnp.int32)
    sent = (send_block[0][:, None] == block_ids[None, :]).astype(jnp.float32)
    outgoing = jnp.einsum("fbc,jb->jfc", node_blocks, sent, precision=lax.Precision.HIGHEST)
    placed = (tile_row[0][:, None] == block_ids[None, :]).astype(jnp.float32)
    local_tiles = tiles[0]
    arrived = lax.all_to_all(outgoing, "dom", split_axis=0, concat_axis=0, tiled=True)
    hopped = hop_terms(arrived, lax.all_gather(local_tiles, "rep", axis=0, tiled=True), placed)
    hop_out = hopped.reshape(feat_cols, row_count)

    per_dev = labels.shape[0]
    per_owner = row_count // dom_size
    owners_here = per_dev // per_owner
    chunk_ids = jnp.arange(owners_here, dtype=jnp.int32)
    rotated = (chunk_ids + dom_at) % owners_here
    node_ids = order[0].reshape(rep_size, owners_here, per_owner)
    node_ids = jnp.take(node_ids, rotated, axis=1).reshape(row_count)
    rows_here = jnp.concatenate([features_t.astype(jnp.bfloat16), hop_out.astype(jnp.bfloat16)], axis=0)
    select = (jnp.arange(row_count, dtype=jnp.int32)[:, None] == node_ids[None, :]).astype(jnp.bfloat16)
    picked = jnp.einsum(
        "fn,nrq->rfq", rows_here, select.reshape(row_count, rep_size, per_dev), preferred_element_type=jnp.float32
    ).astype(jnp.bfloat16)
    got = lax.all_to_all(picked, "rep", split_axis=0, concat_axis=0, tiled=True)
    inputs = got.reshape(rep_size, 2, feat_cols, per_dev).transpose(1, 0, 2, 3).reshape(-1, per_dev)

    def score_pairs(k):
        pairs = []
        for j in range(dom_size):
            for r in range(rep_size):
                owner = (r * owners_here + (k + j) % owners_here) * rep_size + j // owners_here
                pairs.append((j * rep_size + r, owner))
        return pairs

    label_rows = labels.astype(jnp.float32).reshape(owners_here, per_owner)
    sent_at = (dom_at % owners_here - chunk_ids) % owners_here
    label_part = jnp.concatenate(
        [
            lax.ppermute(label_rows[sent_at[k]], ("dom", "rep"), [(b, a) for a, b in score_pairs(k)])
            for k in range(owners_here)
        ]
    )

    pre = lax.dot_general(
        inputs, w_first, (((0,), (0,)), ((), ())), preferred_element_type=jnp.float32
    )
    gate = jax.nn.sigmoid(pre)
    scores = jnp.dot(pre * gate, w_score, precision=lax.Precision.HIGHEST)
    error_term = jax.nn.sigmoid(scores) - label_part
    derivative = gate * (1.0 + pre * (1.0 - gate))
    back = (error_term[:, None] * w_score[None, :] * derivative).astype(jnp.bfloat16)
    local_grad = jnp.dot(inputs, back, preferred_element_type=jnp.float32)
    gradient = reduce_rows(local_grad, dom_size, rep_size)

    score_rows = scores.reshape(owners_here, per_owner)
    returned = jnp.stack(
        [lax.ppermute(score_rows[k], ("dom", "rep"), score_pairs(k)) for k in range(owners_here)]
    )
    own_scores = jnp.take(returned, sent_at, axis=0).reshape(per_dev)
    return (hop_out, own_scores, gradient)


def solution(mesh):
    placed = (
        P("rep", "dom"),
        P("dom", "rep", None, None),
        P("dom", None),
        P("dom", None),
        P("dom", None),
        P(("dom", "rep")),
        P(),
        P(),
    )
    return jax.shard_map(
        on_device,
        mesh=mesh,
        in_specs=placed,
        out_specs=(P("rep", "dom"), P(("dom", "rep")), P("rep", None)),
        check_vma=False,
    )
```
